512 devices in a mesh: section: 2 (over core), req: 64 (over y, z), head: 4 (over x).
Axes of the slice: x: 4, y: 8, z: 8, core: 2. Of those that a mesh axis runs over, the one named last changes fastest.
Arguments:
- embedding_per_slot: bfloat16 [512, 4, 1024], P('req', None, 'head'), may hold values from -6 to 6
- tally_per_slot: int32 [512], P('req'), may hold values from 1 to 4
- slot_requests: int32 [512], replicated, may hold values from 0 to 511, as said below
- memory_per_request: float32 [2, 512, 16, 64, 64], P('section', 'req', 'head'), may hold values from -4 to 4
- previous_step_feature: bfloat16 [2, 512, 1024], P('section', 'req', 'head'), may hold values from -6 to 6
- lag_interpolants: bfloat16 [2, 5, 1024], P('section'), may hold values from 0 to 1
- acceptor_projection: bfloat16 [2, 1024, 1024], P('section', None, 'head'), may hold values from -0.1875 to 0.1875
- address_projection: bfloat16 [2, 1024, 1024], P('section', None, 'head'), may hold values from -0.1875 to 0.1875
- content_projection: bfloat16 [2, 1024, 1024], P('section', None, 'head'), may hold values from -0.1875 to 0.1875
- readout_projection: bfloat16 [2, 1024, 1024], P('section', 'head'), may hold values from -0.1875 to 0.1875
- fading_first_lowrank: bfloat16 [2, 1024, 96], P('section', 'head'), may hold values from -0.1875 to 0.1875
- fading_second_lowrank: bfloat16 [2, 96, 1024], P('section', None, 'head'), may hold values from -0.625 to 0.625
- adapt_first_lowrank: bfloat16 [2, 1024, 96], P('section', 'head'), may hold values from -0.1875 to 0.1875
- adapt_second_lowrank: bfloat16 [2, 96, 1024], P('section', None, 'head'), may hold values from -0.625 to 0.625
- fading_baseline: float32 [2, 1024], P('section', 'head'), may hold values from -4 to 1
- adapt_baseline: float32 [2, 1024], P('section', 'head'), may hold values from -3 to 3
- erasing_address_gains: float32 [2, 1024], P('section', 'head'), may hold values from 0.5 to 1.5
- address_rate_coupling: float32 [2, 1024], P('section', 'head'), may hold values from 0 to 1
- present_extra_gain: float32 [2, 1024], P('section', 'head'), may hold values from -3 to 3
- section_standard_gains: float32 [2, 1024], P('section', 'head'), may hold values from 0.1 to 1.9
- section_standard_shift_terms: float32 [2, 1024], P('section', 'head'), may hold values from -2 to 2
Outputs:
- layer_out: bfloat16 [2, 512, 4, 1024], P('section', 'req', None, 'head')
The draws below stay inside these ranges and needn't reach their ends.
Inputs may be any that keep to these rules, and one draw needn't show every extreme that they name: `slot_requests`: every request appears once. Of one group's 8 arrival slots at most 1 hold requests stored in any one group, and each group holds exactly 1 from some group.
All inputs are finite; a program needn't handle non-finite values.
Results may differ from the reference program's by a relative error of at most 0.02.
Values may be sent and summed in bfloat16 or wider, within the bound.
No kernel may reach another device: no remote copies, remote signals or barrier semaphores. Data moves between devices by JAX's collectives and lax.ppermute only.
A program may use at most 64 MiB of HBM per device.

```python
import jax
import jax.numpy as jnp
from jax import lax

MODEL_DIMENSION = 1024
SUBSPACE_TALLY = 16
SUBSPACE_SIZE = 64
ADAPTER_WIDTH = 96
STEPS = 4
REQ_DEV = 8
R = 512
N_SECTION = 2
N_REQ = 64


def draw_slot_requests(key, part):
    subkeys = jax.random.split(jax.random.fold_in(key, 7), 4)
    first = jax.random.permutation(subkeys[0], N_REQ)
    second = jax.random.permutation(subkeys[1], N_REQ)
    third = jax.random.permutation(subkeys[2], N_REQ)
    within = jax.random.permutation(subkeys[3], REQ_DEV)
    arrive_group = jnp.arange(N_REQ, dtype=jnp.int32)[:, None]
    arrive_slot = jnp.arange(REQ_DEV, dtype=jnp.int32)[None, :]
    home_group = first[(second[arrive_group] + third[arrive_slot % N_REQ]) % N_REQ]
    home_slot = within[arrive_slot] + 0 * arrive_group
    return (home_group * REQ_DEV + home_slot).reshape(-1).astype(jnp.int32)


def with_ends(values, stream_key, smallest, high):
    longest = values.shape.index(max(values.shape))
    spots = []
    for shift in (0, 1):
        where = [jax.random.randint(jax.random.fold_in(stream_key, axis), (), 0, length) for axis, length in enumerate(values.shape)]
        where[longest] = (where[longest] + shift) % values.shape[longest]
        spots.append(tuple(where))
    return values.at[spots[0]].set(smallest).at[spots[1]].set(high)


def block_scale(stream_key, dims, cuts, smallest, largest):
    def one(dim, blocks):
        draws = jax.random.uniform(jax.random.fold_in(jax.random.fold_in(stream_key, 6), dim), (blocks,), jnp.float32, smallest / len(cuts), largest / len(cuts))
        return jnp.repeat(jnp.exp(draws), dims[dim] // blocks).reshape((-1,) + (1,) * (len(dims) - dim - 1))

    loudness = one(*cuts[0])
    for cut in cuts[1:]:
        loudness = loudness * one(*cut)
    return loudness


def scatter_about(own_key, shape, deviation, most, cuts=(), held_as=jnp.bfloat16):
    values = jax.random.normal(own_key, shape, jnp.float32) * deviation
    if len(cuts) > 0:
        values = block_scale(own_key, shape, cuts, -0.22, 0.18) * values
    return jnp.clip(values, min=-most, max=most).astype(held_as)


def setup_inputs(seed: int = 0) -> dict:
    seeds = jax.random.split(jax.random.key(seed), 22)
    embedding_per_slot = scatter_about(seeds[0], (R, STEPS, MODEL_DIMENSION), 1.0, 6.0, ((0, 64), (2, 4)))
    tally_per_slot = with_ends(jax.random.randint(seeds[1], (R,), 1, STEPS + 1), jax.random.fold_in(seeds[1], 1), 1, STEPS).astype(jnp.int32)
    slot_requests = draw_slot_requests(jax.random.fold_in(seeds[21], 71), 0)
    memory_per_request = scatter_about(seeds[3], (N_SECTION, R, SUBSPACE_TALLY, SUBSPACE_SIZE, SUBSPACE_SIZE), 0.5, 4.0, ((0, 2), (1, 64), (2, 4)), jnp.float32)
    previous_step_feature = scatter_about(seeds[4], (N_SECTION, R, MODEL_DIMENSION), 1.0, 6.0, ((0, 2), (1, 64), (2, 4)))
    lag_interpolants = jnp.clip(1.0 * jax.random.uniform(seeds[5], (N_SECTION, 5, MODEL_DIMENSION), jnp.float32) ** block_scale(seeds[5], (N_SECTION, 5, MODEL_DIMENSION), ((0, 2),), -0.2, 0.2), 0.0, 1.0).astype(jnp.bfloat16)
    acceptor_projection = scatter_about(seeds[6], (N_SECTION, MODEL_DIMENSION, SUBSPACE_TALLY * SUBSPACE_SIZE), MODEL_DIMENSION ** -0.5, 0.1875, ((0, 2), (2, 4)))
    address_projection = scatter_about(seeds[7], (N_SECTION, MODEL_DIMENSION, SUBSPACE_TALLY * SUBSPACE_SIZE), MODEL_DIMENSION ** -0.5, 0.1875, ((0, 2), (2, 4)))
    content_projection = scatter_about(seeds[8], (N_SECTION, MODEL_DIMENSION, SUBSPACE_TALLY * SUBSPACE_SIZE), MODEL_DIMENSION ** -0.5, 0.1875, ((0, 2), (2, 4)))
    readout_projection = scatter_about(seeds[9], (N_SECTION, SUBSPACE_TALLY * SUBSPACE_SIZE, MODEL_DIMENSION), (SUBSPACE_TALLY * SUBSPACE_SIZE) ** -0.5, 0.1875, ((0, 2), (1, 4)))
    fading_first_lowrank = scatter_about(seeds[10], (N_SECTION, MODEL_DIMENSION, ADAPTER_WIDTH), MODEL_DIMENSION ** -0.5, 0.1875, ((0, 2), (1, 4)))
    fading_second_lowrank = scatter_about(seeds[11], (N_SECTION, ADAPTER_WIDTH, SUBSPACE_TALLY * SUBSPACE_SIZE), ADAPTER_WIDTH ** -0.5, 0.625, ((0, 2), (2, 4)))
    adapt_first_lowrank = scatter_about(seeds[12], (N_SECTION, MODEL_DIMENSION, ADAPTER_WIDTH), MODEL_DIMENSION ** -0.5, 0.1875, ((0, 2), (1, 4)))
    adapt_second_lowrank = scatter_about(seeds[13], (N_SECTION, ADAPTER_WIDTH, SUBSPACE_TALLY * SUBSPACE_SIZE), ADAPTER_WIDTH ** -0.5, 0.625, ((0, 2), (2, 4)))
    fading_baseline = jnp.clip(-4.0 + 5.0 * jax.random.uniform(seeds[14], (N_SECTION, SUBSPACE_TALLY * SUBSPACE_SIZE), jnp.float32) ** block_scale(seeds[14], (N_SECTION, SUBSPACE_TALLY * SUBSPACE_SIZE), ((0, 2), (1, 4)), -0.2, 0.2), -4.0, 1.0)
    adapt_baseline = jnp.clip(jax.random.uniform(seeds[15], (N_SECTION, SUBSPACE_TALLY * SUBSPACE_SIZE), jnp.float32, -3.0, 3.0) * block_scale(seeds[15], (N_SECTION, SUBSPACE_TALLY * SUBSPACE_SIZE), ((0, 2), (1, 4)), -0.4, 0.0), -3.0, 3.0)
    erasing_address_gains = jnp.clip(0.5 + 1.0 * jax.random.uniform(seeds[16], (N_SECTION, SUBSPACE_TALLY * SUBSPACE_SIZE), jnp.float32) ** block_scale(seeds[16], (N_SECTION, SUBSPACE_TALLY * SUBSPACE_SIZE), ((0, 2), (1, 4)), -0.2, 0.2), 0.5, 1.5)
    address_rate_coupling = jnp.clip(1.0 * jax.random.uniform(seeds[17], (N_SECTION, SUBSPACE_TALLY * SUBSPACE_SIZE), jnp.float32) ** block_scale(seeds[17], (N_SECTION, SUBSPACE_TALLY * SUBSPACE_SIZE), ((0, 2), (1, 4)), -0.2, 0.2), 0.0, 1.0)
    present_extra_gain = scatter_about(seeds[18], (N_SECTION, SUBSPACE_TALLY * SUBSPACE_SIZE), 0.5, 3.0, ((0, 2), (1, 4)), jnp.float32)
    section_standard_gains = jnp.clip(1.0 + 0.18 * jax.random.normal(seeds[19], (N_SECTION, SUBSPACE_TALLY * SUBSPACE_SIZE), jnp.float32), 0.1, 1.9)
    section_standard_shift_terms = scatter_about(seeds[20], (N_SECTION, SUBSPACE_TALLY * SUBSPACE_SIZE), 0.3, 2.0, ((0, 2), (1, 4)), jnp.float32)
    return dict(embedding_per_slot=embedding_per_slot, tally_per_slot=tally_per_slot, slot_requests=slot_requests, memory_per_request=memory_per_request, previous_step_feature=previous_step_feature, lag_interpolants=lag_interpolants, acceptor_projection=acceptor_projection, address_projection=address_projection, content_projection=content_projection, readout_projection=readout_projection, fading_first_lowrank=fading_first_lowrank, fading_second_lowrank=fading_second_lowrank, adapt_first_lowrank=adapt_first_lowrank, adapt_second_lowrank=adapt_second_lowrank, fading_baseline=fading_baseline, adapt_baseline=adapt_baseline, erasing_address_gains=erasing_address_gains, address_rate_coupling=address_rate_coupling, present_extra_gain=present_extra_gain, section_standard_gains=section_standard_gains, section_standard_shift_terms=section_standard_shift_terms)


highest = lax.Precision.HIGHEST

def sequence_recurrence(acceptor_entries, address_entries, content_entries, latent_response, adapt_latent, starting_memory, fading_second_lowrank, adapt_second_lowrank, fading_baseline, adapt_baseline, erasing_address_gains, address_rate_coupling, present_extra_gain, section_standard_gains, section_standard_shift_terms):
    batch_rows = starting_memory.shape[0]
    stored_memory_parts = starting_memory.shape[1]
    subspace_span = starting_memory.shape[2]

    def to_heads(array_in):
        return array_in.reshape(batch_rows, -1, stored_memory_parts, subspace_span)
    log_rate = -jax.nn.softplus(-(fading_baseline + jnp.dot(latent_response, fading_second_lowrank, preferred_element_type=jnp.float32))) - 0.5
    decays = to_heads(jnp.exp(-jnp.exp(log_rate)))
    learning = jax.nn.sigmoid(adapt_baseline + jnp.dot(adapt_latent, adapt_second_lowrank, preferred_element_type=jnp.float32))
    learn_heads = to_heads(learning)
    scaled = to_heads(address_entries * erasing_address_gains)
    normed = scaled / jnp.sqrt(lax.optimization_barrier(jnp.sum(scaled * scaled, axis=-1, keepdims=True)) + 1e-06)
    erasing_address = to_heads(address_entries * (1.0 + (learning - 1.0) * address_rate_coupling))
    acceptor_parts = to_heads(acceptor_entries)
    content_part_lines = to_heads(content_entries)
    states = starting_memory
    readout = []
    for position in range(acceptor_parts.shape[1]):
        pulled = jnp.einsum('rhij,rhj->rhi', states, normed[:, position], precision=highest)
        states = states * decays[:, position][:, :, None, :] - jnp.einsum('rhi,rhj->rhij', pulled, normed[:, position] * learn_heads[:, position], precision=highest) + jnp.einsum('rhi,rhj->rhij', content_part_lines[:, position], erasing_address[:, position], precision=highest)
        readout.append(jnp.einsum('rhij,rhj->rhi', states, acceptor_parts[:, position], precision=highest))
    read_all = jnp.stack(readout, axis=1)
    center = read_all - lax.optimization_barrier(jnp.mean(read_all, axis=-1, keepdims=True))
    variance = lax.optimization_barrier(jnp.mean(center * center, axis=-1, keepdims=True))
    gain_heads = section_standard_gains.reshape(stored_memory_parts, subspace_span)
    bias_heads = section_standard_shift_terms.reshape(stored_memory_parts, subspace_span)
    standardized_parts = center / jnp.sqrt(variance + 0.00064) * gain_heads + bias_heads
    present_extra_term = lax.optimization_barrier(jnp.sum(acceptor_parts * erasing_address * present_extra_gain.reshape(stored_memory_parts, subspace_span), axis=-1, keepdims=True)) * content_part_lines
    return (standardized_parts + present_extra_term).astype(jnp.bfloat16).reshape(-1, stored_memory_parts * subspace_span)

def run_sublevel(lowrank_latent, earlier_entry, starting_memory, lag_interpolants, acceptor_projection, address_projection, content_projection, readout_projection, fading_first_lowrank, fading_second_lowrank, adapt_first_lowrank, adapt_second_lowrank, fading_baseline, adapt_baseline, erasing_address_gains, address_rate_coupling, present_extra_gain, section_standard_gains, section_standard_shift_terms):
    batch_rows, steps_count, model_width = lowrank_latent.shape
    current = lowrank_latent.astype(jnp.float32)
    previous = jnp.concatenate([earlier_entry[:, None, :], lowrank_latent[:, :-1, :]], axis=1).astype(jnp.float32)
    spread = previous - current
    blends = [(current + spread * lag_interpolants[which_mix].astype(jnp.float32)).astype(jnp.bfloat16).reshape(-1, model_width) for which_mix in range(5)]
    acceptor_entries = jnp.dot(blends[0], acceptor_projection, preferred_element_type=jnp.float32)
    address_entries = jnp.dot(blends[2], address_projection, preferred_element_type=jnp.float32)
    content_entries = jnp.dot(blends[3], content_projection, preferred_element_type=jnp.float32)
    latent_response = jnp.tanh(jnp.dot(blends[1], fading_first_lowrank, preferred_element_type=jnp.float32)).astype(jnp.bfloat16)
    adapt_latent = jnp.dot(blends[4], adapt_first_lowrank, preferred_element_type=jnp.float32).astype(jnp.bfloat16)
    lagged_features = sequence_recurrence(acceptor_entries, address_entries, content_entries, latent_response, adapt_latent, starting_memory, fading_second_lowrank, adapt_second_lowrank, fading_baseline, adapt_baseline, erasing_address_gains, address_rate_coupling, present_extra_gain, section_standard_gains, section_standard_shift_terms)
    projected = jnp.dot(lagged_features, readout_projection, preferred_element_type=jnp.float32).reshape(batch_rows, steps_count, model_width)
    return (current + projected).astype(jnp.bfloat16)

def reference(embedding_per_slot, tally_per_slot, slot_requests, memory_per_request, previous_step_feature, lag_interpolants, acceptor_projection, address_projection, content_projection, readout_projection, fading_first_lowrank, fading_second_lowrank, adapt_first_lowrank, adapt_second_lowrank, fading_baseline, adapt_baseline, erasing_address_gains, address_rate_coupling, present_extra_gain, section_standard_gains, section_standard_shift_terms):
    lowrank_latent = embedding_per_slot
    results = []
    for sublevel_number in range(N_SECTION):
        starting_memory = jnp.take(memory_per_request[sublevel_number], slot_requests, axis=0)
        earlier_entry = jnp.take(previous_step_feature[sublevel_number], slot_requests, axis=0)
        lowrank_latent = run_sublevel(lowrank_latent, earlier_entry, starting_memory, lag_interpolants[sublevel_number], acceptor_projection[sublevel_number], address_projection[sublevel_number], content_projection[sublevel_number], readout_projection[sublevel_number], fading_first_lowrank[sublevel_number], fading_second_lowrank[sublevel_number], adapt_first_lowrank[sublevel_number], adapt_second_lowrank[sublevel_number], fading_baseline[sublevel_number], adapt_baseline[sublevel_number], erasing_address_gains[sublevel_number], address_rate_coupling[sublevel_number], present_extra_gain[sublevel_number], section_standard_gains[sublevel_number], section_standard_shift_terms[sublevel_number])
        results.append(lowrank_latent)
    stacked = jnp.stack(results)
    live_mask = jnp.arange(STEPS, dtype=jnp.int32)[None, :] < tally_per_slot[:, None]
    return jnp.where(live_mask[None, :, :, None], stacked, jnp.zeros_like(stacked))
```

```python
import jax
import jax.numpy as jnp
from jax import lax
from jax.sharding import PartitionSpec as P

highest = lax.Precision.HIGHEST


def sequence_recurrence(
    acceptor_entries,
    address_entries,
    content_entries,
    latent_response,
    adapt_latent,
    starting_memory,
    fading_second_lowrank,
    adapt_second_lowrank,
    fading_baseline,
    adapt_baseline,
    erasing_address_gains,
    address_rate_coupling,
    present_extra_gain,
    section_standard_gains,
    section_standard_shift_terms,
):
    batch_rows = starting_memory.shape[0]
    stored_memory_parts = starting_memory.shape[1]
    subspace_span = starting_memory.shape[2]

    def to_heads(array_in):
        return array_in.reshape(batch_rows, -1, stored_memory_parts, subspace_span)

    log_rate = (
        -jax.nn.softplus(
            -(
                fading_baseline
                + jnp.dot(
                    latent_response, fading_second_lowrank, preferred_element_type=jnp.float32
                )
            )
        )
        - 0.5
    )
    decays = to_heads(jnp.exp(-jnp.exp(log_rate)))
    learning = jax.nn.sigmoid(
        adapt_baseline
        + jnp.dot(adapt_latent, adapt_second_lowrank, preferred_element_type=jnp.float32)
    )
    learn_heads = to_heads(learning)
    scaled = to_heads(address_entries * erasing_address_gains)
    normed = scaled / jnp.sqrt(jnp.sum(scaled * scaled, axis=-1, keepdims=True) + 1e-06)
    erasing_address = to_heads(address_entries * (1.0 + (learning - 1.0) * address_rate_coupling))
    acceptor_parts = to_heads(acceptor_entries)
    content_part_lines = to_heads(content_entries)
    states = starting_memory
    readout = []
    for position in range(acceptor_parts.shape[1]):
        pulled = jnp.einsum("rhij,rhj->rhi", states, normed[:, position], precision=highest)
        states = (
            states * decays[:, position][:, :, None, :]
            - jnp.einsum(
                "rhi,rhj->rhij",
                pulled,
                normed[:, position] * learn_heads[:, position],
                precision=highest,
            )
            + jnp.einsum(
                "rhi,rhj->rhij",
                content_part_lines[:, position],
                erasing_address[:, position],
                precision=highest,
            )
        )
        readout.append(
            jnp.einsum("rhij,rhj->rhi", states, acceptor_parts[:, position], precision=highest)
        )
    read_all = jnp.stack(readout, axis=1)
    center = read_all - jnp.mean(read_all, axis=-1, keepdims=True)
    variance = jnp.mean(center * center, axis=-1, keepdims=True)
    gain_heads = section_standard_gains.reshape(stored_memory_parts, subspace_span)
    bias_heads = section_standard_shift_terms.reshape(stored_memory_parts, subspace_span)
    standardized_parts = center / jnp.sqrt(variance + 0.00064) * gain_heads + bias_heads
    present_extra_term = (
        jnp.sum(
            acceptor_parts
            * erasing_address
            * present_extra_gain.reshape(stored_memory_parts, subspace_span),
            axis=-1,
            keepdims=True,
        )
        * content_part_lines
    )
    return (
        (standardized_parts + present_extra_term)
        .astype(jnp.bfloat16)
        .reshape(-1, stored_memory_parts * subspace_span)
    )


def gather_heads(block, axis):
    n = lax.axis_size("head")
    me = lax.axis_index("head")
    pieces = [block]
    for k in range(1, n):
        pieces.append(lax.ppermute(block, "head", [(i, (i + k) % n) for i in range(n)]))
    stacked = jnp.stack(pieces[::-1], axis=0)
    ordered = jnp.roll(stacked, me + 1, axis=0)
    moved = jnp.moveaxis(ordered, 0, axis)
    shape = list(block.shape)
    shape[axis] = shape[axis] * n
    return moved.reshape(shape)


def scatter_heads(partial):
    n = lax.axis_size("head")
    me = lax.axis_index("head")
    width = partial.shape[1] // n
    total = lax.dynamic_slice_in_dim(partial, me * width, width, 1)
    for k in range(1, n):
        chunk = lax.dynamic_slice_in_dim(partial, ((me + k) % n) * width, width, 1)
        total = total + lax.ppermute(chunk, "head", [(i, (i + k) % n) for i in range(n)])
    return total


def hand_over(block):
    n = lax.axis_size("head")
    me = lax.axis_index("head")
    pieces = []
    for k in range(n):
        pieces.append(
            lax.ppermute(block, ("section", "head"), [(i, n + (i + k) % n) for i in range(n)])
        )
    stacked = jnp.stack(pieces[::-1], axis=0)
    ordered = jnp.roll(stacked, me + 1, axis=0)
    moved = jnp.moveaxis(ordered, 0, 2)
    return moved.reshape(block.shape[:2] + (block.shape[2] * n,)), pieces[0]


def run_layer(full_now, full_prev_row, params):
    (
        lag_interpolants,
        acceptor_projection,
        address_projection,
        content_projection,
        readout_projection,
        fading_first_full,
        fading_second_lowrank,
        adapt_first_full,
        adapt_second_lowrank,
        fading_baseline,
        adapt_baseline,
        erasing_address_gains,
        address_rate_coupling,
        present_extra_gain,
        section_standard_gains,
        section_standard_shift_terms,
    ) = params
    batch_rows, steps_count, span_width = full_now.shape
    previous = jnp.concatenate([full_prev_row[:, None, :], full_now[:, :-1, :]], axis=1)
    coef_rows = lag_interpolants.astype(jnp.float32)
    current_piece = full_now.astype(jnp.float32)
    spread_piece = previous.astype(jnp.float32) - current_piece
    blends = [
        (current_piece + spread_piece * coef_rows[which_mix])
        .astype(jnp.bfloat16)
        .reshape(-1, span_width)
        for which_mix in range(5)
    ]
    acceptor_entries = jnp.dot(blends[0], acceptor_projection, preferred_element_type=jnp.float32)
    address_entries = jnp.dot(blends[2], address_projection, preferred_element_type=jnp.float32)
    content_entries = jnp.dot(blends[3], content_projection, preferred_element_type=jnp.float32)
    latent_response = jnp.tanh(
        jnp.dot(blends[1], fading_first_full, preferred_element_type=jnp.float32)
    ).astype(jnp.bfloat16)
    adapt_latent = jnp.dot(blends[4], adapt_first_full, preferred_element_type=jnp.float32).astype(
        jnp.bfloat16
    )
    return acceptor_entries, address_entries, content_entries, latent_response, adapt_latent


def layer_partial(full_now, full_prev_row, starting_memory, params):
    entries = run_layer(full_now, full_prev_row, params)
    lagged_features = sequence_recurrence(
        *entries,
        starting_memory,
        params[6],
        params[8],
        *params[9:],
    )
    return jnp.dot(lagged_features, params[4], preferred_element_type=jnp.float32)


def run_sections(inputs, states_use, last_use, params):
    section_num = lax.axis_index("section")
    batch_rows, steps_count, shard_width = inputs.shape
    full_prev = gather_heads(last_use, 1)
    full_first = gather_heads(inputs, 2)
    partial_first = layer_partial(full_first, full_prev, states_use, params)
    own_first = scatter_heads(partial_first).reshape(batch_rows, steps_count, shard_width)
    first_out = (inputs.astype(jnp.float32) + own_first).astype(jnp.bfloat16)
    full_second, second_in = hand_over(first_out)
    partial_second = layer_partial(full_second, full_prev, states_use, params)
    own_second = scatter_heads(partial_second).reshape(batch_rows, steps_count, shard_width)
    second_out = (second_in.astype(jnp.float32) + own_second).astype(jnp.bfloat16)
    return jnp.where(section_num == 0, first_out, second_out)


def body(
    embedding_per_slot,
    tally_per_slot,
    slot_requests,
    memory_per_request,
    previous_step_feature,
    lag_interpolants,
    acceptor_projection,
    address_projection,
    content_projection,
    readout_projection,
    fading_first_lowrank,
    fading_second_lowrank,
    adapt_first_lowrank,
    adapt_second_lowrank,
    fading_baseline,
    adapt_baseline,
    erasing_address_gains,
    address_rate_coupling,
    present_extra_gain,
    section_standard_gains,
    section_standard_shift_terms,
):
    local_rows = embedding_per_slot.shape[0]
    groups = lax.axis_size("req")
    capacity = (local_rows + groups - 1) // groups
    my_group = lax.axis_index("req")
    slot_ids = jnp.arange(local_rows, dtype=jnp.int32)
    table = slot_requests.reshape(groups, local_rows)
    my_arrivals = lax.dynamic_index_in_dim(table, my_group, 0, keepdims=False)
    home_group = my_arrivals // local_rows
    earlier = slot_ids[None, :] < slot_ids[:, None]
    arrival_rank = jnp.sum(
        ((home_group[:, None] == home_group[None, :]) & earlier).astype(jnp.int32), axis=1
    )
    arrival_slot = home_group * capacity + arrival_rank
    requests = my_group * local_rows + slot_ids
    total_rows = slot_requests.shape[0]
    found = slot_requests[None, :] == requests[:, None]
    positions = jnp.sum(
        jnp.where(found, jnp.arange(total_rows, dtype=jnp.int32)[None, :], 0), axis=1
    )
    source = positions // local_rows
    within = positions % local_rows
    source_homes = jnp.take(table, source, axis=0) // local_rows
    home_rank = jnp.sum(
        ((source_homes == my_group) & (slot_ids[None, :] < within[:, None])).astype(jnp.int32),
        axis=1,
    )
    home_slot = source * capacity + home_rank
    buffer_rows = groups * capacity
    params = (
        lag_interpolants[0],
        acceptor_projection[0],
        address_projection[0],
        content_projection[0],
        readout_projection[0],
        gather_heads(fading_first_lowrank[0], 0),
        fading_second_lowrank[0],
        gather_heads(adapt_first_lowrank[0], 0),
        adapt_second_lowrank[0],
        fading_baseline[0],
        adapt_baseline[0],
        erasing_address_gains[0],
        address_rate_coupling[0],
        present_extra_gain[0],
        section_standard_gains[0],
        section_standard_shift_terms[0],
    )
    states_local = memory_per_request[0]
    last_local = previous_step_feature[0]
    outgoing = (
        jnp.zeros((buffer_rows,) + embedding_per_slot.shape[1:], jnp.bfloat16)
        .at[arrival_slot]
        .set(embedding_per_slot)
    )
    arrived = lax.all_to_all(outgoing, "req", split_axis=0, concat_axis=0, tiled=True)
    inputs = jnp.take(arrived, home_slot, axis=0)
    result = run_sections(inputs, states_local, last_local, params)
    going_back = (
        jnp.zeros((buffer_rows,) + result.shape[1:], jnp.bfloat16).at[home_slot].set(result)
    )
    returned = lax.all_to_all(going_back, "req", split_axis=0, concat_axis=0, tiled=True)
    result = jnp.take(returned, arrival_slot, axis=0)
    live_mask = (
        jnp.arange(embedding_per_slot.shape[1], dtype=jnp.int32)[None, :] < tally_per_slot[:, None]
    )
    return jnp.where(live_mask[:, :, None], result, jnp.zeros_like(result))[None]


def solution(mesh):
    return jax.shard_map(
        body,
        mesh=mesh,
        in_specs=(
            P("req", None, "head"),
            P("req"),
            P(),
            P("section", "req", "head", None, None),
            P("section", "req", "head"),
            P("section", None, None),
            P("section", None, "head"),
            P("section", None, "head"),
            P("section", None, "head"),
            P("section", "head", None),
            P("section", "head", None),
            P("section", None, "head"),
            P("section", "head", None),
            P("section", None, "head"),
            P("section", "head"),
            P("section", "head"),
            P("section", "head"),
            P("section", "head"),
            P("section", "head"),
            P("section", "head"),
            P("section", "head"),
        ),
        out_specs=P("section", "req", None, "head"),
        check_vma=False,
    )
```

```python
import jax
import jax.numpy as jnp
from jax import lax
from jax.experimental import pallas as pl
from jax.experimental.pallas import tpu as pltpu
from jax.sharding import PartitionSpec as P

highest = lax.Precision.HIGHEST


def recurrence_kernel(memory_ref, vector_ref, content_ref, read_ref):
    states = memory_ref[...]
    for position in range(vector_ref.shape[0]):
        decay = vector_ref[position, 0]
        normed = vector_ref[position, 1]
        normed_learn = vector_ref[position, 2]
        erasing = vector_ref[position, 3]
        acceptor = vector_ref[position, 4]
        pulled = jnp.sum(states * normed, axis=-1, keepdims=True)
        states = states * decay - pulled * normed_learn + content_ref[position] * erasing
        read_ref[position] = jnp.sum(states * acceptor, axis=-1, keepdims=True)


def run_recurrence(starting_memory, vectors, content):
    steps = vectors.shape[0]
    blocks, span, _ = starting_memory.shape
    return pl.pallas_call(
        recurrence_kernel,
        out_shape=jax.ShapeDtypeStruct((steps, blocks, span, 1), jnp.float32),
        in_specs=[pl.BlockSpec(memory_space=pltpu.VMEM)] * 3,
        out_specs=pl.BlockSpec(memory_space=pltpu.VMEM),
    )(starting_memory, vectors, content)


def sequence_recurrence(
    acceptor_entries,
    address_entries,
    content_entries,
    latent_response,
    adapt_latent,
    starting_memory,
    fading_second_lowrank,
    adapt_second_lowrank,
    fading_baseline,
    adapt_baseline,
    erasing_address_gains,
    address_rate_coupling,
    present_extra_gain,
    section_standard_gains,
    section_standard_shift_terms,
):
    batch_rows = starting_memory.shape[0]
    stored_memory_parts = starting_memory.shape[1]
    subspace_span = starting_memory.shape[2]

    def to_heads(array_in):
        return array_in.reshape(batch_rows, -1, stored_memory_parts, subspace_span)

    log_rate = (
        -jax.nn.softplus(
            -(
                fading_baseline
                + jnp.dot(
                    latent_response, fading_second_lowrank, preferred_element_type=jnp.float32
                )
            )
        )
        - 0.5
    )
    decays = to_heads(jnp.exp(-jnp.exp(log_rate)))
    learning = jax.nn.sigmoid(
        adapt_baseline
        + jnp.dot(adapt_latent, adapt_second_lowrank, preferred_element_type=jnp.float32)
    )
    learn_heads = to_heads(learning)
    scaled = to_heads(address_entries * erasing_address_gains)
    normed = scaled / jnp.sqrt(jnp.sum(scaled * scaled, axis=-1, keepdims=True) + 1e-06)
    erasing_address = to_heads(address_entries * (1.0 + (learning - 1.0) * address_rate_coupling))
    acceptor_parts = to_heads(acceptor_entries)
    content_part_lines = to_heads(content_entries)
    steps_count = acceptor_parts.shape[1]

    def by_step(array_in):
        return jnp.transpose(array_in, (1, 0, 2, 3)).reshape(
            steps_count, batch_rows * stored_memory_parts, 1, subspace_span
        )

    vectors = jnp.stack(
        [
            by_step(decays),
            by_step(normed),
            by_step(normed * learn_heads),
            by_step(erasing_address),
            by_step(acceptor_parts),
        ],
        axis=1,
    )
    content = by_step(content_part_lines).reshape(
        steps_count, batch_rows * stored_memory_parts, subspace_span, 1
    )
    read = run_recurrence(
        starting_memory.reshape(batch_rows * stored_memory_parts, subspace_span, subspace_span),
        vectors,
        content,
    )
    read_all = jnp.transpose(
        read.reshape(steps_count, batch_rows, stored_memory_parts, subspace_span), (1, 0, 2, 3)
    )
    center = read_all - jnp.mean(read_all, axis=-1, keepdims=True)
    variance = jnp.mean(center * center, axis=-1, keepdims=True)
    gain_heads = section_standard_gains.reshape(stored_memory_parts, subspace_span)
    bias_heads = section_standard_shift_terms.reshape(stored_memory_parts, subspace_span)
    standardized_parts = center / jnp.sqrt(variance + 0.00064) * gain_heads + bias_heads
    present_extra_term = (
        jnp.sum(
            acceptor_parts
            * erasing_address
            * present_extra_gain.reshape(stored_memory_parts, subspace_span),
            axis=-1,
            keepdims=True,
        )
        * content_part_lines
    )
    return (
        (standardized_parts + present_extra_term)
        .astype(jnp.bfloat16)
        .reshape(-1, stored_memory_parts * subspace_span)
    )


def gather_heads(block, axis):
    n = lax.axis_size("head")
    me = lax.axis_index("head")
    pieces = [block]
    for k in range(1, n):
        pieces.append(lax.ppermute(block, "head", [(i, (i + k) % n) for i in range(n)]))
    stacked = jnp.stack(pieces[::-1], axis=0)
    ordered = jnp.roll(stacked, me + 1, axis=0)
    moved = jnp.moveaxis(ordered, 0, axis)
    shape = list(block.shape)
    shape[axis] = shape[axis] * n
    return moved.reshape(shape)


def scatter_heads(partial):
    n = lax.axis_size("head")
    me = lax.axis_index("head")
    width = partial.shape[1] // n
    total = lax.dynamic_slice_in_dim(partial, me * width, width, 1)
    for k in range(1, n):
        chunk = lax.dynamic_slice_in_dim(partial, ((me + k) % n) * width, width, 1)
        total = total + lax.ppermute(chunk, "head", [(i, (i + k) % n) for i in range(n)])
    return total


def hand_over(block):
    n = lax.axis_size("head")
    me = lax.axis_index("head")
    pieces = []
    for k in range(n):
        pieces.append(
            lax.ppermute(block, ("section", "head"), [(i, n + (i + k) % n) for i in range(n)])
        )
    stacked = jnp.stack(pieces[::-1], axis=0)
    ordered = jnp.roll(stacked, me + 1, axis=0)
    moved = jnp.moveaxis(ordered, 0, 2)
    return moved.reshape(block.shape[:2] + (block.shape[2] * n,)), pieces[0]


def run_layer(full_now, full_prev_row, params):
    (
        lag_interpolants,
        acceptor_projection,
        address_projection,
        content_projection,
        readout_projection,
        fading_first_full,
        fading_second_lowrank,
        adapt_first_full,
        adapt_second_lowrank,
        fading_baseline,
        adapt_baseline,
        erasing_address_gains,
        address_rate_coupling,
        present_extra_gain,
        section_standard_gains,
        section_standard_shift_terms,
    ) = params
    batch_rows, steps_count, span_width = full_now.shape
    previous = jnp.concatenate([full_prev_row[:, None, :], full_now[:, :-1, :]], axis=1)
    coef_rows = lag_interpolants.astype(jnp.float32)
    current_piece = full_now.astype(jnp.float32)
    spread_piece = previous.astype(jnp.float32) - current_piece
    blends = [
        (current_piece + spread_piece * coef_rows[which_mix])
        .astype(jnp.bfloat16)
        .reshape(-1, span_width)
        for which_mix in range(5)
    ]
    acceptor_entries = jnp.dot(blends[0], acceptor_projection, preferred_element_type=jnp.float32)
    address_entries = jnp.dot(blends[2], address_projection, preferred_element_type=jnp.float32)
    content_entries = jnp.dot(blends[3], content_projection, preferred_element_type=jnp.float32)
    latent_response = jnp.tanh(
        jnp.dot(blends[1], fading_first_full, preferred_element_type=jnp.float32)
    ).astype(jnp.bfloat16)
    adapt_latent = jnp.dot(blends[4], adapt_first_full, preferred_element_type=jnp.float32).astype(
        jnp.bfloat16
    )
    return acceptor_entries, address_entries, content_entries, latent_response, adapt_latent


def layer_partial(full_now, full_prev_row, starting_memory, params):
    entries = run_layer(full_now, full_prev_row, params)
    lagged_features = sequence_recurrence(
        *entries,
        starting_memory,
        params[6],
        params[8],
        *params[9:],
    )
    return jnp.dot(lagged_features, params[4], preferred_element_type=jnp.float32)


def gather_start(last_use, fading_first, adapt_first):
    n = lax.axis_size("head")
    packed = jnp.concatenate([fading_first.reshape(-1), adapt_first.reshape(-1), last_use.reshape(-1)])
    whole = gather_heads(packed, 0).reshape(n, -1)
    first_size = fading_first.size
    fading_full = whole[:, :first_size].reshape((n * fading_first.shape[0],) + fading_first.shape[1:])
    adapt_full = whole[:, first_size : 2 * first_size].reshape(fading_full.shape)
    prev_full = jnp.transpose(
        whole[:, 2 * first_size :].reshape((n,) + last_use.shape), (1, 0, 2)
    ).reshape(last_use.shape[0], n * last_use.shape[1])
    return prev_full, fading_full, adapt_full


def run_sections(inputs, states_use, last_use, params):
    section_num = lax.axis_index("section")
    batch_rows, steps_count, shard_width = inputs.shape
    full_prev, fading_full, adapt_full = gather_start(last_use, params[5], params[7])
    params = params[:5] + (fading_full, params[6], adapt_full) + params[8:]
    full_first = gather_heads(inputs, 2)
    partial_first = layer_partial(full_first, full_prev, states_use, params)
    own_first = scatter_heads(partial_first).reshape(batch_rows, steps_count, shard_width)
    first_out = (inputs.astype(jnp.float32) + own_first).astype(jnp.bfloat16)
    full_second, second_in = hand_over(first_out)
    partial_second = layer_partial(full_second, full_prev, states_use, params)
    own_second = scatter_heads(partial_second).reshape(batch_rows, steps_count, shard_width)
    second_out = (second_in.astype(jnp.float32) + own_second).astype(jnp.bfloat16)
    return jnp.where(section_num == 0, first_out, second_out)


def body(
    embedding_per_slot,
    tally_per_slot,
    slot_requests,
    memory_per_request,
    previous_step_feature,
    lag_interpolants,
    acceptor_projection,
    address_projection,
    content_projection,
    readout_projection,
    fading_first_lowrank,
    fading_second_lowrank,
    adapt_first_lowrank,
    adapt_second_lowrank,
    fading_baseline,
    adapt_baseline,
    erasing_address_gains,
    address_rate_coupling,
    present_extra_gain,
    section_standard_gains,
    section_standard_shift_terms,
):
    local_rows = embedding_per_slot.shape[0]
    groups = lax.axis_size("req")
    capacity = (local_rows + groups - 1) // groups
    my_group = lax.axis_index("req")
    slot_ids = jnp.arange(local_rows, dtype=jnp.int32)
    table = slot_requests.reshape(groups, local_rows)
    my_arrivals = lax.dynamic_index_in_dim(table, my_group, 0, keepdims=False)
    home_group = my_arrivals // local_rows
    earlier = slot_ids[None, :] < slot_ids[:, None]
    arrival_rank = jnp.sum(
        ((home_group[:, None] == home_group[None, :]) & earlier).astype(jnp.int32), axis=1
    )
    arrival_slot = home_group * capacity + arrival_rank
    requests = my_group * local_rows + slot_ids
    total_rows = slot_requests.shape[0]
    found = slot_requests[None, :] == requests[:, None]
    positions = jnp.sum(
        jnp.where(found, jnp.arange(total_rows, dtype=jnp.int32)[None, :], 0), axis=1
    )
    source = positions // local_rows
    within = positions % local_rows
    source_homes = jnp.take(table, source, axis=0) // local_rows
    home_rank = jnp.sum(
        ((source_homes == my_group) & (slot_ids[None, :] < within[:, None])).astype(jnp.int32),
        axis=1,
    )
    home_slot = source * capacity + home_rank
    buffer_rows = groups * capacity
    params = (
        lag_interpolants[0],
        acceptor_projection[0],
        address_projection[0],
        content_projection[0],
        readout_projection[0],
        fading_first_lowrank[0],
        fading_second_lowrank[0],
        adapt_first_lowrank[0],
        adapt_second_lowrank[0],
        fading_baseline[0],
        adapt_baseline[0],
        erasing_address_gains[0],
        address_rate_coupling[0],
        present_extra_gain[0],
        section_standard_gains[0],
        section_standard_shift_terms[0],
    )
    states_local = memory_per_request[0]
    last_local = previous_step_feature[0]
    outgoing = (
        jnp.zeros((buffer_rows,) + embedding_per_slot.shape[1:], jnp.bfloat16)
        .at[arrival_slot]
        .set(embedding_per_slot)
    )
    arrived = lax.all_to_all(outgoing, "req", split_axis=0, concat_axis=0, tiled=True)
    inputs = jnp.take(arrived, home_slot, axis=0)
    result = run_sections(inputs, states_local, last_local, params)
    going_back = (
        jnp.zeros((buffer_rows,) + result.shape[1:], jnp.bfloat16).at[home_slot].set(result)
    )
    returned = lax.all_to_all(going_back, "req", split_axis=0, concat_axis=0, tiled=True)
    result = jnp.take(returned, arrival_slot, axis=0)
    live_mask = (
        jnp.arange(embedding_per_slot.shape[1], dtype=jnp.int32)[None, :] < tally_per_slot[:, None]
    )
    return jnp.where(live_mask[:, :, None], result, jnp.zeros_like(result))[None]


def solution(mesh):
    return jax.shard_map(
        body,
        mesh=mesh,
        in_specs=(
            P("req", None, "head"),
            P("req"),
            P(),
            P("section", "req", "head", None, None),
            P("section", "req", "head"),
            P("section", None, None),
            P("section", None, "head"),
            P("section", None, "head"),
            P("section", None, "head"),
            P("section", "head", None),
            P("section", "head", None),
            P("section", None, "head"),
            P("section", "head", None),
            P("section", None, "head"),
            P("section", "head"),
            P("section", "head"),
            P("section", "head"),
            P("section", "head"),
            P("section", "head"),
            P("section", "head"),
            P("section", "head"),
        ),
        out_specs=P("section", "req", None, "head"),
        check_vma=False,
    )
```

```python
import jax
import jax.numpy as jnp
from jax import lax
from jax.experimental import pallas as pl
from jax.experimental.pallas import tpu as pltpu
from jax.sharding import PartitionSpec as P

highest = lax.Precision.HIGHEST


def recurrence_kernel(memory_ref, vector_ref, content_ref, read_ref):
    states = memory_ref[...]
    for position in range(vector_ref.shape[0]):
        decay = vector_ref[position, 0]
        normed = vector_ref[position, 1]
        normed_learn = vector_ref[position, 2]
        erasing = vector_ref[position, 3]
        acceptor = vector_ref[position, 4]
        pulled = jnp.sum(states * normed, axis=-1, keepdims=True)
        states = states * decay - pulled * normed_learn + content_ref[position] * erasing
        read_ref[position] = jnp.sum(states * acceptor, axis=-1, keepdims=True)


def run_recurrence(starting_memory, vectors, content):
    steps = vectors.shape[0]
    blocks, span, _ = starting_memory.shape
    return pl.pallas_call(
        recurrence_kernel,
        out_shape=jax.ShapeDtypeStruct((steps, blocks, span, 1), jnp.float32),
        in_specs=[pl.BlockSpec(memory_space=pltpu.VMEM)] * 3,
        out_specs=pl.BlockSpec(memory_space=pltpu.VMEM),
    )(starting_memory, vectors, content)


def sequence_recurrence(
    acceptor_entries,
    address_entries,
    content_entries,
    latent_response,
    adapt_latent,
    starting_memory,
    fading_second_lowrank,
    adapt_second_lowrank,
    fading_baseline,
    adapt_baseline,
    erasing_address_gains,
    address_rate_coupling,
    present_extra_gain,
    section_standard_gains,
    section_standard_shift_terms,
):
    batch_rows = starting_memory.shape[0]
    stored_memory_parts = starting_memory.shape[1]
    subspace_span = starting_memory.shape[2]

    def to_heads(array_in):
        return array_in.reshape(batch_rows, -1, stored_memory_parts, subspace_span)

    log_rate = (
        -jax.nn.softplus(
            -(
                fading_baseline
                + jnp.dot(
                    latent_response, fading_second_lowrank, preferred_element_type=jnp.float32
                )
            )
        )
        - 0.5
    )
    decays = to_heads(jnp.exp(-jnp.exp(log_rate)))
    learning = jax.nn.sigmoid(
        adapt_baseline
        + jnp.dot(adapt_latent, adapt_second_lowrank, preferred_element_type=jnp.float32)
    )
    learn_heads = to_heads(learning)
    scaled = to_heads(address_entries * erasing_address_gains)
    normed = scaled / jnp.sqrt(jnp.sum(scaled * scaled, axis=-1, keepdims=True) + 1e-06)
    erasing_address = to_heads(address_entries * (1.0 + (learning - 1.0) * address_rate_coupling))
    acceptor_parts = to_heads(acceptor_entries)
    content_part_lines = to_heads(content_entries)
    steps_count = acceptor_parts.shape[1]

    def by_step(array_in):
        return jnp.transpose(array_in, (1, 0, 2, 3)).reshape(
            steps_count, batch_rows * stored_memory_parts, 1, subspace_span
        )

    vectors = jnp.stack(
        [
            by_step(decays),
            by_step(normed),
            by_step(normed * learn_heads),
            by_step(erasing_address),
            by_step(acceptor_parts),
        ],
        axis=1,
    )
    content = by_step(content_part_lines).reshape(
        steps_count, batch_rows * stored_memory_parts, subspace_span, 1
    )
    read = run_recurrence(
        starting_memory.reshape(batch_rows * stored_memory_parts, subspace_span, subspace_span),
        vectors,
        content,
    )
    read_all = jnp.transpose(
        read.reshape(steps_count, batch_rows, stored_memory_parts, subspace_span), (1, 0, 2, 3)
    )
    center = read_all - jnp.mean(read_all, axis=-1, keepdims=True)
    variance = jnp.mean(center * center, axis=-1, keepdims=True)
    gain_heads = section_standard_gains.reshape(stored_memory_parts, subspace_span)
    bias_heads = section_standard_shift_terms.reshape(stored_memory_parts, subspace_span)
    standardized_parts = center / jnp.sqrt(variance + 0.00064) * gain_heads + bias_heads
    present_extra_term = (
        jnp.sum(
            acceptor_parts
            * erasing_address
            * present_extra_gain.reshape(stored_memory_parts, subspace_span),
            axis=-1,
            keepdims=True,
        )
        * content_part_lines
    )
    return (
        (standardized_parts + present_extra_term)
        .astype(jnp.bfloat16)
        .reshape(-1, stored_memory_parts * subspace_span)
    )


def in_device_order(pieces):
    n = len(pieces)
    me = lax.axis_index("head")
    ordered = []
    for d in range(n):
        chosen = pieces[0]
        for k in range(1, n):
            chosen = jnp.where((me - k) % n == d, pieces[k], chosen)
        ordered.append(chosen)
    return ordered


def gather_heads(block):
    n = lax.axis_size("head")
    pieces = [block]
    for k in range(1, n):
        pieces.append(lax.ppermute(block, "head", [(i, (i + k) % n) for i in range(n)]))
    return in_device_order(pieces)


def scatter_heads(partial):
    n = lax.axis_size("head")
    me = lax.axis_index("head")
    width = partial.shape[1] // n
    total = lax.dynamic_slice_in_dim(partial, me * width, width, 1)
    for k in range(1, n):
        chunk = lax.dynamic_slice_in_dim(partial, ((me + k) % n) * width, width, 1)
        total = total + lax.ppermute(chunk, "head", [(i, (i + k) % n) for i in range(n)])
    return total


def hand_over(partial):
    n = lax.axis_size("head")
    total = None
    for k in range(n):
        piece = lax.ppermute(partial, ("section", "head"), [(i, n + (i + k) % n) for i in range(n)])
        total = piece if total is None else total + piece
    return total


def hand_back(block):
    n = lax.axis_size("head")
    return lax.ppermute(block, ("section", "head"), [(n + i, i) for i in range(n)])


def run_layer(full_now, full_prev_row, params):
    (
        lag_interpolants,
        acceptor_projection,
        address_projection,
        content_projection,
        readout_projection,
        fading_first_full,
        fading_second_lowrank,
        adapt_first_full,
        adapt_second_lowrank,
        fading_baseline,
        adapt_baseline,
        erasing_address_gains,
        address_rate_coupling,
        present_extra_gain,
        section_standard_gains,
        section_standard_shift_terms,
    ) = params
    batch_rows, steps_count, span_width = full_now.shape
    previous = jnp.concatenate([full_prev_row[:, None, :], full_now[:, :-1, :]], axis=1)
    coef_rows = lag_interpolants.astype(jnp.float32)
    current_piece = full_now.astype(jnp.float32)
    spread_piece = previous.astype(jnp.float32) - current_piece
    blends = [
        (current_piece + spread_piece * coef_rows[which_mix])
        .astype(jnp.bfloat16)
        .reshape(-1, span_width)
        for which_mix in range(5)
    ]
    acceptor_entries = jnp.dot(blends[0], acceptor_projection, preferred_element_type=jnp.float32)
    address_entries = jnp.dot(blends[2], address_projection, preferred_element_type=jnp.float32)
    content_entries = jnp.dot(blends[3], content_projection, preferred_element_type=jnp.float32)
    latent_response = jnp.tanh(
        jnp.dot(blends[1], fading_first_full, preferred_element_type=jnp.float32)
    ).astype(jnp.bfloat16)
    adapt_latent = jnp.dot(blends[4], adapt_first_full, preferred_element_type=jnp.float32).astype(
        jnp.bfloat16
    )
    return acceptor_entries, address_entries, content_entries, latent_response, adapt_latent


def layer_partial(full_now, full_prev_row, starting_memory, params):
    entries = run_layer(full_now, full_prev_row, params)
    lagged_features = sequence_recurrence(
        *entries,
        starting_memory,
        params[6],
        params[8],
        *params[9:],
    )
    return jnp.dot(lagged_features, params[4], preferred_element_type=jnp.float32)


def run_sections(inputs, states_use, last_use, params):
    section_num = lax.axis_index("section")
    n = lax.axis_size("head")
    batch_rows, steps_count, shard_width = inputs.shape
    fading_first, adapt_first = params[5], params[7]
    sizes = [inputs.size, last_use.size, fading_first.size, adapt_first.size]
    packed = jnp.concatenate(
        [inputs.reshape(-1), last_use.reshape(-1), fading_first.reshape(-1), adapt_first.reshape(-1)]
    )
    ordered = gather_heads(packed)
    cuts = [0]
    for size in sizes:
        cuts.append(cuts[-1] + size)

    def joined(index, shape, axis):
        parts = [piece[cuts[index] : cuts[index + 1]].reshape(shape) for piece in ordered]
        return jnp.concatenate(parts, axis=axis)

    full_first = joined(0, inputs.shape, 2)
    full_prev = joined(1, last_use.shape, 1)
    fading_full = joined(2, fading_first.shape, 0)
    adapt_full = joined(3, adapt_first.shape, 0)
    params = params[:5] + (fading_full, params[6], adapt_full) + params[8:]
    partial_first = layer_partial(full_first, full_prev, states_use, params)
    total_first = hand_over(partial_first)
    full_second = (
        full_first.astype(jnp.float32) + total_first.reshape(full_first.shape)
    ).astype(jnp.bfloat16)
    me = lax.axis_index("head")
    second_in = lax.dynamic_slice_in_dim(full_second, me * shard_width, shard_width, 2)
    first_out = hand_back(second_in)
    partial_second = layer_partial(full_second, full_prev, states_use, params)
    own_second = scatter_heads(partial_second).reshape(batch_rows, steps_count, shard_width)
    second_out = (second_in.astype(jnp.float32) + own_second).astype(jnp.bfloat16)
    return jnp.where(section_num == 0, first_out, second_out)


def body(
    embedding_per_slot,
    tally_per_slot,
    slot_requests,
    memory_per_request,
    previous_step_feature,
    lag_interpolants,
    acceptor_projection,
    address_projection,
    content_projection,
    readout_projection,
    fading_first_lowrank,
    fading_second_lowrank,
    adapt_first_lowrank,
    adapt_second_lowrank,
    fading_baseline,
    adapt_baseline,
    erasing_address_gains,
    address_rate_coupling,
    present_extra_gain,
    section_standard_gains,
    section_standard_shift_terms,
):
    local_rows = embedding_per_slot.shape[0]
    groups = lax.axis_size("req")
    capacity = (local_rows + groups - 1) // groups
    my_group = lax.axis_index("req")
    slot_ids = jnp.arange(local_rows, dtype=jnp.int32)
    table = slot_requests.reshape(groups, local_rows)
    my_arrivals = lax.dynamic_index_in_dim(table, my_group, 0, keepdims=False)
    home_group = my_arrivals // local_rows
    earlier = slot_ids[None, :] < slot_ids[:, None]
    arrival_rank = jnp.sum(
        ((home_group[:, None] == home_group[None, :]) & earlier).astype(jnp.int32), axis=1
    )
    arrival_slot = home_group * capacity + arrival_rank
    requests = my_group * local_rows + slot_ids
    total_rows = slot_requests.shape[0]
    found = slot_requests[None, :] == requests[:, None]
    positions = jnp.sum(
        jnp.where(found, jnp.arange(total_rows, dtype=jnp.int32)[None, :], 0), axis=1
    )
    source = positions // local_rows
    within = positions % local_rows
    source_homes = jnp.take(table, source, axis=0) // local_rows
    home_rank = jnp.sum(
        ((source_homes == my_group) & (slot_ids[None, :] < within[:, None])).astype(jnp.int32),
        axis=1,
    )
    home_slot = source * capacity + home_rank
    buffer_rows = groups * capacity
    params = (
        lag_interpolants.reshape(lag_interpolants.shape[1:]),
        acceptor_projection.reshape(acceptor_projection.shape[1:]),
        address_projection.reshape(address_projection.shape[1:]),
        content_projection.reshape(content_projection.shape[1:]),
        readout_projection.reshape(readout_projection.shape[1:]),
        fading_first_lowrank.reshape(fading_first_lowrank.shape[1:]),
        fading_second_lowrank.reshape(fading_second_lowrank.shape[1:]),
        adapt_first_lowrank.reshape(adapt_first_lowrank.shape[1:]),
        adapt_second_lowrank.reshape(adapt_second_lowrank.shape[1:]),
        fading_baseline.reshape(fading_baseline.shape[1:]),
        adapt_baseline.reshape(adapt_baseline.shape[1:]),
        erasing_address_gains.reshape(erasing_address_gains.shape[1:]),
        address_rate_coupling.reshape(address_rate_coupling.shape[1:]),
        present_extra_gain.reshape(present_extra_gain.shape[1:]),
        section_standard_gains.reshape(section_standard_gains.shape[1:]),
        section_standard_shift_terms.reshape(section_standard_shift_terms.shape[1:]),
    )
    states_local = memory_per_request.reshape(memory_per_request.shape[1:])
    last_local = previous_step_feature.reshape(previous_step_feature.shape[1:])
    outgoing = (
        jnp.zeros((buffer_rows,) + embedding_per_slot.shape[1:], jnp.bfloat16)
        .at[arrival_slot]
        .set(embedding_per_slot)
    )
    arrived = lax.all_to_all(outgoing, "req", split_axis=0, concat_axis=0, tiled=True)
    inputs = jnp.take(arrived, home_slot, axis=0)
    result = run_sections(inputs, states_local, last_local, params)
    going_back = (
        jnp.zeros((buffer_rows,) + result.shape[1:], jnp.bfloat16).at[home_slot].set(result)
    )
    returned = lax.all_to_all(going_back, "req", split_axis=0, concat_axis=0, tiled=True)
    result = jnp.take(returned, arrival_slot, axis=0)
    live_mask = (
        jnp.arange(embedding_per_slot.shape[1], dtype=jnp.int32)[None, :] < tally_per_slot[:, None]
    )
    return jnp.where(live_mask[:, :, None], result, jnp.zeros_like(result))[None]


def solution(mesh):
    return jax.shard_map(
        body,
        mesh=mesh,
        in_specs=(
            P("req", None, "head"),
            P("req"),
            P(),
            P("section", "req", "head", None, None),
            P("section", "req", "head"),
            P("section", None, None),
            P("section", None, "head"),
            P("section", None, "head"),
            P("section", None, "head"),
            P("section", "head", None),
            P("section", "head", None),
            P("section", None, "head"),
            P("section", "head", None),
            P("section", None, "head"),
            P("section", "head"),
            P("section", "head"),
            P("section", "head"),
            P("section", "head"),
            P("section", "head"),
            P("section", "head"),
            P("section", "head"),
        ),
        out_specs=P("section", "req", None, "head"),
        check_vma=False,
    )
```

```python
import jax
import jax.numpy as jnp
from jax import lax
from jax.experimental import pallas as pl
from jax.experimental.pallas import tpu as pltpu
from jax.sharding import PartitionSpec as P

highest = lax.Precision.HIGHEST


def recurrence_kernel(memory_ref, vector_ref, content_ref, read_ref):
    states = memory_ref[...]
    for position in range(vector_ref.shape[0]):
        decay = vector_ref[position, 0]
        normed = vector_ref[position, 1]
        normed_learn = vector_ref[position, 2]
        erasing = vector_ref[position, 3]
        acceptor = vector_ref[position, 4]
        pulled = jnp.sum(states * normed, axis=-1, keepdims=True)
        states = states * decay - pulled * normed_learn + content_ref[position] * erasing
        read_ref[position] = jnp.sum(states * acceptor, axis=-1, keepdims=True)


def run_recurrence(starting_memory, vectors, content):
    steps = vectors.shape[0]
    blocks, span, _ = starting_memory.shape
    return pl.pallas_call(
        recurrence_kernel,
        out_shape=jax.ShapeDtypeStruct((steps, blocks, span, 1), jnp.float32),
        in_specs=[pl.BlockSpec(memory_space=pltpu.VMEM)] * 3,
        out_specs=pl.BlockSpec(memory_space=pltpu.VMEM),
    )(starting_memory, vectors, content)


def sequence_recurrence(
    acceptor_entries,
    address_entries,
    content_entries,
    latent_response,
    adapt_latent,
    starting_memory,
    fading_second_lowrank,
    adapt_second_lowrank,
    fading_baseline,
    adapt_baseline,
    erasing_address_gains,
    address_rate_coupling,
    present_extra_gain,
    section_standard_gains,
    section_standard_shift_terms,
):
    batch_rows = starting_memory.shape[0]
    stored_memory_parts = starting_memory.shape[1]
    subspace_span = starting_memory.shape[2]

    def to_heads(array_in):
        return array_in.reshape(batch_rows, -1, stored_memory_parts, subspace_span)

    log_rate = (
        -jax.nn.softplus(
            -(
                fading_baseline
                + jnp.dot(
                    latent_response, fading_second_lowrank, preferred_element_type=jnp.float32
                )
            )
        )
        - 0.5
    )
    decays = to_heads(jnp.exp(-jnp.exp(log_rate)))
    learning = jax.nn.sigmoid(
        adapt_baseline
        + jnp.dot(adapt_latent, adapt_second_lowrank, preferred_element_type=jnp.float32)
    )
    learn_heads = to_heads(learning)
    scaled = to_heads(address_entries * erasing_address_gains)
    normed = scaled / jnp.sqrt(jnp.sum(scaled * scaled, axis=-1, keepdims=True) + 1e-06)
    erasing_address = to_heads(address_entries * (1.0 + (learning - 1.0) * address_rate_coupling))
    acceptor_parts = to_heads(acceptor_entries)
    content_part_lines = to_heads(content_entries)
    steps_count = acceptor_parts.shape[1]

    def by_step(array_in):
        return jnp.transpose(array_in, (1, 0, 2, 3)).reshape(
            steps_count, batch_rows * stored_memory_parts, 1, subspace_span
        )

    vectors = jnp.stack(
        [
            by_step(decays),
            by_step(normed),
            by_step(normed * learn_heads),
            by_step(erasing_address),
            by_step(acceptor_parts),
        ],
        axis=1,
    )
    content = by_step(content_part_lines).reshape(
        steps_count, batch_rows * stored_memory_parts, subspace_span, 1
    )
    read = run_recurrence(
        starting_memory.reshape(batch_rows * stored_memory_parts, subspace_span, subspace_span),
        vectors,
        content,
    )
    read_all = jnp.transpose(
        read.reshape(steps_count, batch_rows, stored_memory_parts, subspace_span), (1, 0, 2, 3)
    )
    center = read_all - jnp.mean(read_all, axis=-1, keepdims=True)
    variance = jnp.mean(center * center, axis=-1, keepdims=True)
    gain_heads = section_standard_gains.reshape(stored_memory_parts, subspace_span)
    bias_heads = section_standard_shift_terms.reshape(stored_memory_parts, subspace_span)
    standardized_parts = center / jnp.sqrt(variance + 0.00064) * gain_heads + bias_heads
    present_extra_term = (
        jnp.sum(
            acceptor_parts
            * erasing_address
            * present_extra_gain.reshape(stored_memory_parts, subspace_span),
            axis=-1,
            keepdims=True,
        )
        * content_part_lines
    )
    return (
        (standardized_parts + present_extra_term)
        .astype(jnp.bfloat16)
        .reshape(-1, stored_memory_parts * subspace_span)
    )


def in_device_order(pieces):
    n = len(pieces)
    me = lax.axis_index("head")
    ordered = []
    for d in range(n):
        chosen = pieces[0]
        for k in range(1, n):
            chosen = jnp.where((me - k) % n == d, pieces[k], chosen)
        ordered.append(chosen)
    return ordered


def gather_heads(block):
    n = lax.axis_size("head")
    copies = jnp.broadcast_to(block[None], (n,) + block.shape)
    arrived = lax.all_to_all(copies, "head", split_axis=0, concat_axis=0, tiled=True)
    return [arrived[d] for d in range(n)]


def scatter_heads(partial):
    n = lax.axis_size("head")
    rows, columns = partial.shape
    chunks = jnp.transpose(partial.reshape(rows, n, columns // n), (1, 0, 2))
    arrived = lax.all_to_all(chunks, "head", split_axis=0, concat_axis=0, tiled=True)
    total = arrived[0]
    for d in range(1, n):
        total = total + arrived[d]
    return total


def hand_over(partial):
    n = lax.axis_size("head")
    total = None
    for k in range(n):
        piece = lax.ppermute(partial, ("section", "head"), [(i, n + (i + k) % n) for i in range(n)])
        total = piece if total is None else total + piece
    return total


def hand_back(block):
    n = lax.axis_size("head")
    return lax.ppermute(block, ("section", "head"), [(n + i, i) for i in range(n)])


def run_layer(full_now, full_prev_row, params):
    (
        lag_interpolants,
        acceptor_projection,
        address_projection,
        content_projection,
        readout_projection,
        fading_first_full,
        fading_second_lowrank,
        adapt_first_full,
        adapt_second_lowrank,
        fading_baseline,
        adapt_baseline,
        erasing_address_gains,
        address_rate_coupling,
        present_extra_gain,
        section_standard_gains,
        section_standard_shift_terms,
    ) = params
    batch_rows, steps_count, span_width = full_now.shape
    previous = jnp.concatenate([full_prev_row[:, None, :], full_now[:, :-1, :]], axis=1)
    coef_rows = lag_interpolants.astype(jnp.float32)
    current_piece = full_now.astype(jnp.float32)
    spread_piece = previous.astype(jnp.float32) - current_piece
    blends = [
        (current_piece + spread_piece * coef_rows[which_mix])
        .astype(jnp.bfloat16)
        .reshape(-1, span_width)
        for which_mix in range(5)
    ]
    acceptor_entries = jnp.dot(blends[0], acceptor_projection, preferred_element_type=jnp.float32)
    address_entries = jnp.dot(blends[2], address_projection, preferred_element_type=jnp.float32)
    content_entries = jnp.dot(blends[3], content_projection, preferred_element_type=jnp.float32)
    latent_response = jnp.tanh(
        jnp.dot(blends[1], fading_first_full, preferred_element_type=jnp.float32)
    ).astype(jnp.bfloat16)
    adapt_latent = jnp.dot(blends[4], adapt_first_full, preferred_element_type=jnp.float32).astype(
        jnp.bfloat16
    )
    return acceptor_entries, address_entries, content_entries, latent_response, adapt_latent


def layer_partial(full_now, full_prev_row, starting_memory, params):
    entries = run_layer(full_now, full_prev_row, params)
    lagged_features = sequence_recurrence(
        *entries,
        starting_memory,
        params[6],
        params[8],
        *params[9:],
    )
    return jnp.dot(lagged_features, params[4], preferred_element_type=jnp.float32)


def run_sections(inputs, states_use, last_use, params):
    section_num = lax.axis_index("section")
    n = lax.axis_size("head")
    batch_rows, steps_count, shard_width = inputs.shape
    fading_first, adapt_first = params[5], params[7]
    sizes = [inputs.size, last_use.size, fading_first.size, adapt_first.size]
    packed = jnp.concatenate(
        [inputs.reshape(-1), last_use.reshape(-1), fading_first.reshape(-1), adapt_first.reshape(-1)]
    )
    ordered = gather_heads(packed)
    cuts = [0]
    for size in sizes:
        cuts.append(cuts[-1] + size)

    def joined(index, shape, axis):
        parts = [piece[cuts[index] : cuts[index + 1]].reshape(shape) for piece in ordered]
        return jnp.concatenate(parts, axis=axis)

    full_first = joined(0, inputs.shape, 2)
    full_prev = joined(1, last_use.shape, 1)
    fading_full = joined(2, fading_first.shape, 0)
    adapt_full = joined(3, adapt_first.shape, 0)
    params = params[:5] + (fading_full, params[6], adapt_full) + params[8:]
    partial_first = layer_partial(full_first, full_prev, states_use, params)
    total_first = hand_over(partial_first)
    full_second = (
        full_first.astype(jnp.float32) + total_first.reshape(full_first.shape)
    ).astype(jnp.bfloat16)
    me = lax.axis_index("head")
    second_in = lax.dynamic_slice_in_dim(full_second, me * shard_width, shard_width, 2)
    first_out = hand_back(second_in)
    partial_second = layer_partial(full_second, full_prev, states_use, params)
    own_second = scatter_heads(partial_second).reshape(batch_rows, steps_count, shard_width)
    second_out = (second_in.astype(jnp.float32) + own_second).astype(jnp.bfloat16)
    return jnp.where(section_num == 0, first_out, second_out)


def body(
    embedding_per_slot,
    tally_per_slot,
    slot_requests,
    memory_per_request,
    previous_step_feature,
    lag_interpolants,
    acceptor_projection,
    address_projection,
    content_projection,
    readout_projection,
    fading_first_lowrank,
    fading_second_lowrank,
    adapt_first_lowrank,
    adapt_second_lowrank,
    fading_baseline,
    adapt_baseline,
    erasing_address_gains,
    address_rate_coupling,
    present_extra_gain,
    section_standard_gains,
    section_standard_shift_terms,
):
    local_rows = embedding_per_slot.shape[0]
    groups = lax.axis_size("req")
    capacity = (local_rows + groups - 1) // groups
    my_group = lax.axis_index("req")
    slot_ids = jnp.arange(local_rows, dtype=jnp.int32)
    table = slot_requests.reshape(groups, local_rows)
    my_arrivals = lax.dynamic_index_in_dim(table, my_group, 0, keepdims=False)
    home_group = my_arrivals // local_rows
    earlier = slot_ids[None, :] < slot_ids[:, None]
    arrival_rank = jnp.sum(
        ((home_group[:, None] == home_group[None, :]) & earlier).astype(jnp.int32), axis=1
    )
    arrival_slot = home_group * capacity + arrival_rank
    requests = my_group * local_rows + slot_ids
    total_rows = slot_requests.shape[0]
    found = slot_requests[None, :] == requests[:, None]
    positions = jnp.sum(
        jnp.where(found, jnp.arange(total_rows, dtype=jnp.int32)[None, :], 0), axis=1
    )
    source = positions // local_rows
    within = positions % local_rows
    source_homes = jnp.take(table, source, axis=0) // local_rows
    home_rank = jnp.sum(
        ((source_homes == my_group) & (slot_ids[None, :] < within[:, None])).astype(jnp.int32),
        axis=1,
    )
    home_slot = source * capacity + home_rank
    buffer_rows = groups * capacity
    params = (
        lag_interpolants.reshape(lag_interpolants.shape[1:]),
        acceptor_projection.reshape(acceptor_projection.shape[1:]),
        address_projection.reshape(address_projection.shape[1:]),
        content_projection.reshape(content_projection.shape[1:]),
        readout_projection.reshape(readout_projection.shape[1:]),
        fading_first_lowrank.reshape(fading_first_lowrank.shape[1:]),
        fading_second_lowrank.reshape(fading_second_lowrank.shape[1:]),
        adapt_first_lowrank.reshape(adapt_first_lowrank.shape[1:]),
        adapt_second_lowrank.reshape(adapt_second_lowrank.shape[1:]),
        fading_baseline.reshape(fading_baseline.shape[1:]),
        adapt_baseline.reshape(adapt_baseline.shape[1:]),
        erasing_address_gains.reshape(erasing_address_gains.shape[1:]),
        address_rate_coupling.reshape(address_rate_coupling.shape[1:]),
        present_extra_gain.reshape(present_extra_gain.shape[1:]),
        section_standard_gains.reshape(section_standard_gains.shape[1:]),
        section_standard_shift_terms.reshape(section_standard_shift_terms.shape[1:]),
    )
    states_local = memory_per_request.reshape(memory_per_request.shape[1:])
    last_local = previous_step_feature.reshape(previous_step_feature.shape[1:])
    outgoing = (
        jnp.zeros((buffer_rows,) + embedding_per_slot.shape[1:], jnp.bfloat16)
        .at[arrival_slot]
        .set(embedding_per_slot)
    )
    arrived = lax.all_to_all(outgoing, "req", split_axis=0, concat_axis=0, tiled=True)
    inputs = jnp.take(arrived, home_slot, axis=0)
    result = run_sections(inputs, states_local, last_local, params)
    going_back = (
        jnp.zeros((buffer_rows,) + result.shape[1:], jnp.bfloat16).at[home_slot].set(result)
    )
    returned = lax.all_to_all(going_back, "req", split_axis=0, concat_axis=0, tiled=True)
    result = jnp.take(returned, arrival_slot, axis=0)
    live_mask = (
        jnp.arange(embedding_per_slot.shape[1], dtype=jnp.int32)[None, :] < tally_per_slot[:, None]
    )
    return jnp.where(live_mask[:, :, None], result, jnp.zeros_like(result))[None]


def solution(mesh):
    return jax.shard_map(
        body,
        mesh=mesh,
        in_specs=(
            P("req", None, "head"),
            P("req"),
            P(),
            P("section", "req", "head", None, None),
            P("section", "req", "head"),
            P("section", None, None),
            P("section", None, "head"),
            P("section", None, "head"),
            P("section", None, "head"),
            P("section", "head", None),
            P("section", "head", None),
            P("section", None, "head"),
            P("section", "head", None),
            P("section", None, "head"),
            P("section", "head"),
            P("section", "head"),
            P("section", "head"),
            P("section", "head"),
            P("section", "head"),
            P("section", "head"),
            P("section", "head"),
        ),
        out_specs=P("section", "req", None, "head"),
        check_vma=False,
    )
```

```python
import jax
import jax.numpy as jnp
from jax import lax
from jax.experimental import pallas as pl
from jax.experimental.pallas import tpu as pltpu
from jax.sharding import PartitionSpec as P

highest = lax.Precision.HIGHEST


def recurrence_kernel(memory_ref, vector_ref, content_ref, read_ref):
    steps, _, blocks, _ = vector_ref.shape
    for block in range(blocks):
        states = memory_ref[block]
        for position in range(steps):
            row = slice(block, block + 1)
            column = slice(position * blocks + block, position * blocks + block + 1)
            decay = vector_ref[position, 0, row, :]
            normed = vector_ref[position, 1, row, :]
            normed_learn = vector_ref[position, 2, row, :]
            erasing = vector_ref[position, 3, row, :]
            acceptor = vector_ref[position, 4, row, :]
            content = content_ref[:, column]
            pulled = jnp.sum(states * normed, axis=1, keepdims=True)
            states = states * decay - pulled * normed_learn + content * erasing
            read_ref[:, column] = jnp.sum(states * acceptor, axis=1, keepdims=True)


def run_recurrence(starting_memory, vectors, content):
    return pl.pallas_call(
        recurrence_kernel,
        out_shape=jax.ShapeDtypeStruct(content.shape, jnp.float32),
        in_specs=[pl.BlockSpec(memory_space=pltpu.VMEM)] * 3,
        out_specs=pl.BlockSpec(memory_space=pltpu.VMEM),
    )(starting_memory, vectors, content)


def sequence_recurrence(
    acceptor_entries,
    address_entries,
    content_entries,
    latent_response,
    adapt_latent,
    starting_memory,
    fading_second_lowrank,
    adapt_second_lowrank,
    fading_baseline,
    adapt_baseline,
    erasing_address_gains,
    address_rate_coupling,
    present_extra_gain,
    section_standard_gains,
    section_standard_shift_terms,
):
    batch_rows = starting_memory.shape[0]
    stored_memory_parts = starting_memory.shape[1]
    subspace_span = starting_memory.shape[2]

    def to_heads(array_in):
        return array_in.reshape(batch_rows, -1, stored_memory_parts, subspace_span)

    log_rate = (
        -jax.nn.softplus(
            -(
                fading_baseline
                + jnp.dot(
                    latent_response, fading_second_lowrank, preferred_element_type=jnp.float32
                )
            )
        )
        - 0.5
    )
    decays = to_heads(jnp.exp(-jnp.exp(log_rate)))
    learning = jax.nn.sigmoid(
        adapt_baseline
        + jnp.dot(adapt_latent, adapt_second_lowrank, preferred_element_type=jnp.float32)
    )
    learn_heads = to_heads(learning)
    scaled = to_heads(address_entries * erasing_address_gains)
    normed = scaled / jnp.sqrt(jnp.sum(scaled * scaled, axis=-1, keepdims=True) + 1e-06)
    erasing_address = to_heads(address_entries * (1.0 + (learning - 1.0) * address_rate_coupling))
    acceptor_parts = to_heads(acceptor_entries)
    content_part_lines = to_heads(content_entries)
    steps_count = acceptor_parts.shape[1]

    def by_step(array_in):
        return jnp.transpose(array_in, (1, 0, 2, 3)).reshape(
            steps_count, batch_rows * stored_memory_parts, subspace_span
        )

    vectors = jnp.stack(
        [
            by_step(decays),
            by_step(normed),
            by_step(normed * learn_heads),
            by_step(erasing_address),
            by_step(acceptor_parts),
        ],
        axis=1,
    )
    content = jnp.transpose(content_part_lines, (3, 1, 0, 2)).reshape(subspace_span, -1)
    read = run_recurrence(
        starting_memory.reshape(batch_rows * stored_memory_parts, subspace_span, subspace_span),
        vectors,
        content,
    )
    read_all = jnp.transpose(
        read.reshape(subspace_span, steps_count, batch_rows, stored_memory_parts), (2, 1, 3, 0)
    )
    center = read_all - jnp.mean(read_all, axis=-1, keepdims=True)
    variance = jnp.mean(center * center, axis=-1, keepdims=True)
    gain_heads = section_standard_gains.reshape(stored_memory_parts, subspace_span)
    bias_heads = section_standard_shift_terms.reshape(stored_memory_parts, subspace_span)
    standardized_parts = center / jnp.sqrt(variance + 0.00064) * gain_heads + bias_heads
    present_extra_term = (
        jnp.sum(
            acceptor_parts
            * erasing_address
            * present_extra_gain.reshape(stored_memory_parts, subspace_span),
            axis=-1,
            keepdims=True,
        )
        * content_part_lines
    )
    return (
        (standardized_parts + present_extra_term)
        .astype(jnp.bfloat16)
        .reshape(-1, stored_memory_parts * subspace_span)
    )


def in_device_order(pieces):
    n = len(pieces)
    me = lax.axis_index("head")
    ordered = []
    for d in range(n):
        chosen = pieces[0]
        for k in range(1, n):
            chosen = jnp.where((me - k) % n == d, pieces[k], chosen)
        ordered.append(chosen)
    return ordered


def gather_heads(block):
    n = lax.axis_size("head")
    pieces = [block]
    for k in range(1, n):
        pieces.append(lax.ppermute(block, "head", [(i, (i + k) % n) for i in range(n)]))
    return in_device_order(pieces)


def scatter_heads(partial):
    n = lax.axis_size("head")
    me = lax.axis_index("head")
    width = partial.shape[1] // n
    total = lax.dynamic_slice_in_dim(partial, me * width, width, 1)
    for k in range(1, n):
        chunk = lax.dynamic_slice_in_dim(partial, ((me + k) % n) * width, width, 1)
        total = total + lax.ppermute(chunk, "head", [(i, (i + k) % n) for i in range(n)])
    return total


def hand_over(partial):
    n = lax.axis_size("head")
    total = None
    for k in range(n):
        piece = lax.ppermute(partial, ("section", "head"), [(i, n + (i + k) % n) for i in range(n)])
        total = piece if total is None else total + piece
    return total


def hand_back(block):
    n = lax.axis_size("head")
    return lax.ppermute(block, ("section", "head"), [(n + i, i) for i in range(n)])


def run_layer(full_now, full_prev_row, params):
    (
        lag_interpolants,
        acceptor_projection,
        address_projection,
        content_projection,
        readout_projection,
        fading_first_full,
        fading_second_lowrank,
        adapt_first_full,
        adapt_second_lowrank,
        fading_baseline,
        adapt_baseline,
        erasing_address_gains,
        address_rate_coupling,
        present_extra_gain,
        section_standard_gains,
        section_standard_shift_terms,
    ) = params
    batch_rows, steps_count, span_width = full_now.shape
    previous = jnp.concatenate([full_prev_row[:, None, :], full_now[:, :-1, :]], axis=1)
    coef_rows = lag_interpolants.astype(jnp.float32)
    current_piece = full_now.astype(jnp.float32)
    spread_piece = previous.astype(jnp.float32) - current_piece
    blends = [
        (current_piece + spread_piece * coef_rows[which_mix])
        .astype(jnp.bfloat16)
        .reshape(-1, span_width)
        for which_mix in range(5)
    ]
    acceptor_entries = jnp.dot(blends[0], acceptor_projection, preferred_element_type=jnp.float32)
    address_entries = jnp.dot(blends[2], address_projection, preferred_element_type=jnp.float32)
    content_entries = jnp.dot(blends[3], content_projection, preferred_element_type=jnp.float32)
    latent_response = jnp.tanh(
        jnp.dot(blends[1], fading_first_full, preferred_element_type=jnp.float32)
    ).astype(jnp.bfloat16)
    adapt_latent = jnp.dot(blends[4], adapt_first_full, preferred_element_type=jnp.float32).astype(
        jnp.bfloat16
    )
    return acceptor_entries, address_entries, content_entries, latent_response, adapt_latent


def layer_partial(full_now, full_prev_row, starting_memory, params):
    entries = run_layer(full_now, full_prev_row, params)
    lagged_features = sequence_recurrence(
        *entries,
        starting_memory,
        params[6],
        params[8],
        *params[9:],
    )
    return jnp.dot(lagged_features, params[4], preferred_element_type=jnp.float32)


def run_sections(inputs, states_use, last_use, params):
    section_num = lax.axis_index("section")
    n = lax.axis_size("head")
    batch_rows, steps_count, shard_width = inputs.shape
    fading_first, adapt_first = params[5], params[7]
    sizes = [inputs.size, last_use.size, fading_first.size, adapt_first.size]
    packed = jnp.concatenate(
        [inputs.reshape(-1), last_use.reshape(-1), fading_first.reshape(-1), adapt_first.reshape(-1)]
    )
    ordered = gather_heads(packed)
    cuts = [0]
    for size in sizes:
        cuts.append(cuts[-1] + size)

    def joined(index, shape, axis):
        parts = [piece[cuts[index] : cuts[index + 1]].reshape(shape) for piece in ordered]
        return jnp.concatenate(parts, axis=axis)

    full_first = joined(0, inputs.shape, 2)
    full_prev = joined(1, last_use.shape, 1)
    fading_full = joined(2, fading_first.shape, 0)
    adapt_full = joined(3, adapt_first.shape, 0)
    params = params[:5] + (fading_full, params[6], adapt_full) + params[8:]
    partial_first = layer_partial(full_first, full_prev, states_use, params)
    total_first = hand_over(partial_first)
    full_second = (
        full_first.astype(jnp.float32) + total_first.reshape(full_first.shape)
    ).astype(jnp.bfloat16)
    me = lax.axis_index("head")
    second_in = lax.dynamic_slice_in_dim(full_second, me * shard_width, shard_width, 2)
    first_out = hand_back(second_in)
    partial_second = layer_partial(full_second, full_prev, states_use, params)
    own_second = scatter_heads(partial_second).reshape(batch_rows, steps_count, shard_width)
    second_out = (second_in.astype(jnp.float32) + own_second).astype(jnp.bfloat16)
    return jnp.where(section_num == 0, first_out, second_out)


def body(
    embedding_per_slot,
    tally_per_slot,
    slot_requests,
    memory_per_request,
    previous_step_feature,
    lag_interpolants,
    acceptor_projection,
    address_projection,
    content_projection,
    readout_projection,
    fading_first_lowrank,
    fading_second_lowrank,
    adapt_first_lowrank,
    adapt_second_lowrank,
    fading_baseline,
    adapt_baseline,
    erasing_address_gains,
    address_rate_coupling,
    present_extra_gain,
    section_standard_gains,
    section_standard_shift_terms,
):
    local_rows = embedding_per_slot.shape[0]
    groups = lax.axis_size("req")
    capacity = (local_rows + groups - 1) // groups
    my_group = lax.axis_index("req")
    slot_ids = jnp.arange(local_rows, dtype=jnp.int32)
    table = slot_requests.reshape(groups, local_rows)
    my_arrivals = lax.dynamic_index_in_dim(table, my_group, 0, keepdims=False)
    home_group = my_arrivals // local_rows
    earlier = slot_ids[None, :] < slot_ids[:, None]
    arrival_rank = jnp.sum(
        ((home_group[:, None] == home_group[None, :]) & earlier).astype(jnp.int32), axis=1
    )
    arrival_slot = home_group * capacity + arrival_rank
    requests = my_group * local_rows + slot_ids
    total_rows = slot_requests.shape[0]
    found = slot_requests[None, :] == requests[:, None]
    positions = jnp.sum(
        jnp.where(found, jnp.arange(total_rows, dtype=jnp.int32)[None, :], 0), axis=1
    )
    source = positions // local_rows
    within = positions % local_rows
    source_homes = jnp.take(table, source, axis=0) // local_rows
    home_rank = jnp.sum(
        ((source_homes == my_group) & (slot_ids[None, :] < within[:, None])).astype(jnp.int32),
        axis=1,
    )
    home_slot = source * capacity + home_rank
    buffer_rows = groups * capacity
    params = (
        lag_interpolants.reshape(lag_interpolants.shape[1:]),
        acceptor_projection.reshape(acceptor_projection.shape[1:]),
        address_projection.reshape(address_projection.shape[1:]),
        content_projection.reshape(content_projection.shape[1:]),
        readout_projection.reshape(readout_projection.shape[1:]),
        fading_first_lowrank.reshape(fading_first_lowrank.shape[1:]),
        fading_second_lowrank.reshape(fading_second_lowrank.shape[1:]),
        adapt_first_lowrank.reshape(adapt_first_lowrank.shape[1:]),
        adapt_second_lowrank.reshape(adapt_second_lowrank.shape[1:]),
        fading_baseline,
        adapt_baseline,
        erasing_address_gains,
        address_rate_coupling,
        present_extra_gain,
        section_standard_gains,
        section_standard_shift_terms,
    )
    states_local = memory_per_request.reshape(memory_per_request.shape[1:])
    last_local = previous_step_feature.reshape(previous_step_feature.shape[1:])
    outgoing = (
        jnp.zeros((buffer_rows,) + embedding_per_slot.shape[1:], jnp.bfloat16)
        .at[arrival_slot]
        .set(embedding_per_slot)
    )
    arrived = lax.all_to_all(outgoing, "req", split_axis=0, concat_axis=0, tiled=True)
    inputs = jnp.take(arrived, home_slot, axis=0)
    result = run_sections(inputs, states_local, last_local, params)
    going_back = (
        jnp.zeros((buffer_rows,) + result.shape[1:], jnp.bfloat16).at[home_slot].set(result)
    )
    returned = lax.all_to_all(going_back, "req", split_axis=0, concat_axis=0, tiled=True)
    result = jnp.take(returned, arrival_slot, axis=0)
    live_mask = (
        jnp.arange(embedding_per_slot.shape[1], dtype=jnp.int32)[None, :] < tally_per_slot[:, None]
    )
    return jnp.where(live_mask[:, :, None], result, jnp.zeros_like(result))[None]


def solution(mesh):
    return jax.shard_map(
        body,
        mesh=mesh,
        in_specs=(
            P("req", None, "head"),
            P("req"),
            P(),
            P("section", "req", "head", None, None),
            P("section", "req", "head"),
            P("section", None, None),
            P("section", None, "head"),
            P("section", None, "head"),
            P("section", None, "head"),
            P("section", "head", None),
            P("section", "head", None),
            P("section", None, "head"),
            P("section", "head", None),
            P("section", None, "head"),
            P("section", "head"),
            P("section", "head"),
            P("section", "head"),
            P("section", "head"),
            P("section", "head"),
            P("section", "head"),
            P("section", "head"),
        ),
        out_specs=P("section", "req", None, "head"),
        check_vma=False,
    )
```

```python
import jax
import jax.numpy as jnp
from jax import lax
from jax.experimental import pallas as pl
from jax.experimental.pallas import tpu as pltpu
from jax.sharding import PartitionSpec as P

highest = lax.Precision.HIGHEST


def recurrence_kernel(memory_ref, vector_ref, content_ref, read_ref):
    states = memory_ref[...]
    for position in range(vector_ref.shape[0]):
        decay = vector_ref[position, 0]
        normed = vector_ref[position, 1]
        normed_learn = vector_ref[position, 2]
        erasing = vector_ref[position, 3]
        acceptor = vector_ref[position, 4]
        pulled = jnp.sum(states * normed, axis=-1, keepdims=True)
        states = states * decay - pulled * normed_learn + content_ref[position] * erasing
        read_ref[position] = jnp.sum(states * acceptor, axis=-1, keepdims=True)


def run_recurrence(starting_memory, vectors, content):
    steps = vectors.shape[0]
    blocks, span, _ = starting_memory.shape
    return pl.pallas_call(
        recurrence_kernel,
        out_shape=jax.ShapeDtypeStruct((steps, blocks, span, 1), jnp.float32),
        in_specs=[pl.BlockSpec(memory_space=pltpu.VMEM)] * 3,
        out_specs=pl.BlockSpec(memory_space=pltpu.VMEM),
    )(starting_memory, vectors, content)


def sequence_recurrence(
    acceptor_entries,
    address_entries,
    content_entries,
    latent_response,
    adapt_latent,
    starting_memory,
    fading_second_lowrank,
    adapt_second_lowrank,
    fading_baseline,
    adapt_baseline,
    erasing_address_gains,
    address_rate_coupling,
    present_extra_gain,
    section_standard_gains,
    section_standard_shift_terms,
):
    batch_rows = starting_memory.shape[0]
    stored_memory_parts = starting_memory.shape[1]
    subspace_span = starting_memory.shape[2]

    def to_heads(array_in):
        return array_in.reshape(batch_rows, -1, stored_memory_parts, subspace_span)

    log_rate = (
        -jax.nn.softplus(
            -(
                fading_baseline
                + jnp.dot(
                    latent_response, fading_second_lowrank, preferred_element_type=jnp.float32
                )
            )
        )
        - 0.5
    )
    decays = to_heads(jnp.exp(-jnp.exp(log_rate)))
    learning = jax.nn.sigmoid(
        adapt_baseline
        + jnp.dot(adapt_latent, adapt_second_lowrank, preferred_element_type=jnp.float32)
    )
    learn_heads = to_heads(learning)
    scaled = to_heads(address_entries * erasing_address_gains)
    normed = scaled / jnp.sqrt(jnp.sum(scaled * scaled, axis=-1, keepdims=True) + 1e-06)
    erasing_address = to_heads(address_entries * (1.0 + (learning - 1.0) * address_rate_coupling))
    acceptor_parts = to_heads(acceptor_entries)
    content_part_lines = to_heads(content_entries)
    steps_count = acceptor_parts.shape[1]

    def by_step(array_in):
        return jnp.transpose(array_in, (1, 0, 2, 3)).reshape(
            steps_count, batch_rows * stored_memory_parts, 1, subspace_span
        )

    vectors = jnp.stack(
        [
            by_step(decays),
            by_step(normed),
            by_step(normed * learn_heads),
            by_step(erasing_address),
            by_step(acceptor_parts),
        ],
        axis=1,
    )
    content = by_step(content_part_lines).reshape(
        steps_count, batch_rows * stored_memory_parts, subspace_span, 1
    )
    read = run_recurrence(
        starting_memory.reshape(batch_rows * stored_memory_parts, subspace_span, subspace_span),
        vectors,
        content,
    )
    read_all = jnp.transpose(
        read.reshape(steps_count, batch_rows, stored_memory_parts, subspace_span), (1, 0, 2, 3)
    )
    center = read_all - jnp.mean(read_all, axis=-1, keepdims=True)
    variance = jnp.mean(center * center, axis=-1, keepdims=True)
    gain_heads = section_standard_gains.reshape(stored_memory_parts, subspace_span)
    bias_heads = section_standard_shift_terms.reshape(stored_memory_parts, subspace_span)
    standardized_parts = center / jnp.sqrt(variance + 0.00064) * gain_heads + bias_heads
    present_extra_term = (
        jnp.sum(
            acceptor_parts
            * erasing_address
            * present_extra_gain.reshape(stored_memory_parts, subspace_span),
            axis=-1,
            keepdims=True,
        )
        * content_part_lines
    )
    return (
        (standardized_parts + present_extra_term)
        .astype(jnp.bfloat16)
        .reshape(-1, stored_memory_parts * subspace_span)
    )


def in_device_order(pieces):
    n = len(pieces)
    me = lax.axis_index("head")
    ordered = []
    for d in range(n):
        chosen = pieces[0]
        for k in range(1, n):
            chosen = jnp.where((me - k) % n == d, pieces[k], chosen)
        ordered.append(chosen)
    return ordered


def gather_heads(block):
    n = lax.axis_size("head")
    pieces = [block]
    for k in range(1, n):
        pieces.append(lax.ppermute(block, "head", [(i, (i + k) % n) for i in range(n)]))
    return in_device_order(pieces)


def scatter_heads(partial):
    n = lax.axis_size("head")
    me = lax.axis_index("head")
    width = partial.shape[1] // n
    total = lax.dynamic_slice_in_dim(partial, me * width, width, 1)
    for k in range(1, n):
        chunk = lax.dynamic_slice_in_dim(partial, ((me + k) % n) * width, width, 1)
        total = total + lax.ppermute(chunk, "head", [(i, (i + k) % n) for i in range(n)])
    return total


def hand_over(partial):
    n = lax.axis_size("head")
    total = None
    for k in range(n):
        piece = lax.ppermute(partial, ("section", "head"), [(i, n + (i + k) % n) for i in range(n)])
        total = piece if total is None else total + piece
    return total


def hand_back(block):
    n = lax.axis_size("head")
    return lax.ppermute(block, ("section", "head"), [(n + i, i) for i in range(n)])


def run_layer(full_now, full_prev_row, params):
    (
        lag_interpolants,
        acceptor_projection,
        address_projection,
        content_projection,
        readout_projection,
        fading_first_full,
        fading_second_lowrank,
        adapt_first_full,
        adapt_second_lowrank,
        fading_baseline,
        adapt_baseline,
        erasing_address_gains,
        address_rate_coupling,
        present_extra_gain,
        section_standard_gains,
        section_standard_shift_terms,
    ) = params
    batch_rows, steps_count, span_width = full_now.shape
    previous = jnp.concatenate([full_prev_row[:, None, :], full_now[:, :-1, :]], axis=1)
    coef_rows = lag_interpolants.astype(jnp.float32)
    current_piece = full_now.astype(jnp.float32)
    spread_piece = previous.astype(jnp.float32) - current_piece
    blends = [
        (current_piece + spread_piece * coef_rows[which_mix])
        .astype(jnp.bfloat16)
        .reshape(-1, span_width)
        for which_mix in range(5)
    ]
    acceptor_entries = jnp.dot(blends[0], acceptor_projection, preferred_element_type=jnp.float32)
    address_entries = jnp.dot(blends[2], address_projection, preferred_element_type=jnp.float32)
    content_entries = jnp.dot(blends[3], content_projection, preferred_element_type=jnp.float32)
    latent_response = jnp.tanh(
        jnp.dot(blends[1], fading_first_full, preferred_element_type=jnp.float32)
    ).astype(jnp.bfloat16)
    adapt_latent = jnp.dot(blends[4], adapt_first_full, preferred_element_type=jnp.float32).astype(
        jnp.bfloat16
    )
    return acceptor_entries, address_entries, content_entries, latent_response, adapt_latent


def layer_partial(full_now, full_prev_row, starting_memory, params):
    entries = run_layer(full_now, full_prev_row, params)
    lagged_features = sequence_recurrence(
        *entries,
        starting_memory,
        params[6],
        params[8],
        *params[9:],
    )
    return jnp.dot(lagged_features, params[4], preferred_element_type=jnp.float32)


def run_sections(inputs, states_use, last_use, params):
    section_num = lax.axis_index("section")
    n = lax.axis_size("head")
    batch_rows, steps_count, shard_width = inputs.shape
    fading_first, adapt_first = params[5], params[7]
    sizes = [inputs.size, last_use.size, fading_first.size, adapt_first.size]
    packed = jnp.concatenate(
        [inputs.reshape(-1), last_use.reshape(-1), fading_first.reshape(-1), adapt_first.reshape(-1)]
    )
    ordered = gather_heads(packed)
    cuts = [0]
    for size in sizes:
        cuts.append(cuts[-1] + size)

    def joined(index, shape, axis):
        parts = [piece[cuts[index] : cuts[index + 1]].reshape(shape) for piece in ordered]
        return jnp.concatenate(parts, axis=axis)

    full_first = joined(0, inputs.shape, 2)
    full_prev = joined(1, last_use.shape, 1)
    fading_full = joined(2, fading_first.shape, 0)
    adapt_full = joined(3, adapt_first.shape, 0)
    params = params[:5] + (fading_full, params[6], adapt_full) + params[8:]
    partial_first = layer_partial(full_first, full_prev, states_use, params)
    total_first = hand_over(partial_first)
    full_second = (
        full_first.astype(jnp.float32) + total_first.reshape(full_first.shape)
    ).astype(jnp.bfloat16)
    me = lax.axis_index("head")
    second_in = lax.dynamic_slice_in_dim(full_second, me * shard_width, shard_width, 2)
    first_out = hand_back(second_in)
    partial_second = layer_partial(full_second, full_prev, states_use, params)
    own_second = scatter_heads(partial_second).reshape(batch_rows, steps_count, shard_width)
    second_out = (second_in.astype(jnp.float32) + own_second).astype(jnp.bfloat16)
    return jnp.where(section_num == 0, first_out, second_out)


def body(
    embedding_per_slot,
    tally_per_slot,
    slot_requests,
    memory_per_request,
    previous_step_feature,
    lag_interpolants,
    acceptor_projection,
    address_projection,
    content_projection,
    readout_projection,
    fading_first_lowrank,
    fading_second_lowrank,
    adapt_first_lowrank,
    adapt_second_lowrank,
    fading_baseline,
    adapt_baseline,
    erasing_address_gains,
    address_rate_coupling,
    present_extra_gain,
    section_standard_gains,
    section_standard_shift_terms,
):
    local_rows = embedding_per_slot.shape[0]
    groups = lax.axis_size("req")
    capacity = (local_rows + groups - 1) // groups
    my_group = lax.axis_index("req")
    slot_ids = jnp.arange(local_rows, dtype=jnp.int32)
    table = slot_requests.reshape(groups, local_rows)
    my_arrivals = lax.dynamic_index_in_dim(table, my_group, 0, keepdims=False)
    home_group = my_arrivals // local_rows
    earlier = slot_ids[None, :] < slot_ids[:, None]
    arrival_rank = jnp.sum(
        ((home_group[:, None] == home_group[None, :]) & earlier).astype(jnp.int32), axis=1
    )
    arrival_slot = home_group * capacity + arrival_rank
    requests = my_group * local_rows + slot_ids
    total_rows = slot_requests.shape[0]
    found = slot_requests[None, :] == requests[:, None]
    positions = jnp.sum(
        jnp.where(found, jnp.arange(total_rows, dtype=jnp.int32)[None, :], 0), axis=1
    )
    source = positions // local_rows
    within = positions % local_rows
    source_homes = jnp.take(table, source, axis=0) // local_rows
    home_rank = jnp.sum(
        ((source_homes == my_group) & (slot_ids[None, :] < within[:, None])).astype(jnp.int32),
        axis=1,
    )
    home_slot = source * capacity + home_rank
    buffer_rows = groups * capacity
    params = (
        lag_interpolants.reshape(lag_interpolants.shape[1:]),
        acceptor_projection.reshape(acceptor_projection.shape[1:]),
        address_projection.reshape(address_projection.shape[1:]),
        content_projection.reshape(content_projection.shape[1:]),
        readout_projection.reshape(readout_projection.shape[1:]),
        fading_first_lowrank.reshape(fading_first_lowrank.shape[1:]),
        fading_second_lowrank.reshape(fading_second_lowrank.shape[1:]),
        adapt_first_lowrank.reshape(adapt_first_lowrank.shape[1:]),
        adapt_second_lowrank.reshape(adapt_second_lowrank.shape[1:]),
        fading_baseline,
        adapt_baseline,
        erasing_address_gains,
        address_rate_coupling,
        present_extra_gain,
        section_standard_gains,
        section_standard_shift_terms,
    )
    states_local = memory_per_request.reshape(memory_per_request.shape[1:])
    last_local = previous_step_feature.reshape(previous_step_feature.shape[1:])
    outgoing = (
        jnp.zeros((buffer_rows,) + embedding_per_slot.shape[1:], jnp.bfloat16)
        .at[arrival_slot]
        .set(embedding_per_slot)
    )
    arrived = lax.all_to_all(outgoing, "req", split_axis=0, concat_axis=0, tiled=True)
    inputs = jnp.take(arrived, home_slot, axis=0)
    result = run_sections(inputs, states_local, last_local, params)
    going_back = (
        jnp.zeros((buffer_rows,) + result.shape[1:], jnp.bfloat16).at[home_slot].set(result)
    )
    returned = lax.all_to_all(going_back, "req", split_axis=0, concat_axis=0, tiled=True)
    result = jnp.take(returned, arrival_slot, axis=0)
    live_mask = (
        jnp.arange(embedding_per_slot.shape[1], dtype=jnp.int32)[None, :] < tally_per_slot[:, None]
    )
    return jnp.where(live_mask[:, :, None], result, jnp.zeros_like(result))[None]


def solution(mesh):
    return jax.shard_map(
        body,
        mesh=mesh,
        in_specs=(
            P("req", None, "head"),
            P("req"),
            P(),
            P("section", "req", "head", None, None),
            P("section", "req", "head"),
            P("section", None, None),
            P("section", None, "head"),
            P("section", None, "head"),
            P("section", None, "head"),
            P("section", "head", None),
            P("section", "head", None),
            P("section", None, "head"),
            P("section", "head", None),
            P("section", None, "head"),
            P("section", "head"),
            P("section", "head"),
            P("section", "head"),
            P("section", "head"),
            P("section", "head"),
            P("section", "head"),
            P("section", "head"),
        ),
        out_specs=P("section", "req", None, "head"),
        check_vma=False,
    )
```

```python
import jax
import jax.numpy as jnp
from jax import lax
from jax.experimental import pallas as pl
from jax.experimental.pallas import tpu as pltpu
from jax.sharding import PartitionSpec as P

highest = lax.Precision.HIGHEST


def recurrence_kernel(memory_ref, vector_ref, content_ref, read_ref):
    states = memory_ref[...]
    for position in range(vector_ref.shape[0]):
        decay = vector_ref[position, 0]
        normed = vector_ref[position, 1]
        normed_learn = vector_ref[position, 2]
        erasing = vector_ref[position, 3]
        acceptor = vector_ref[position, 4]
        pulled = jnp.sum(states * normed, axis=-1, keepdims=True)
        states = states * decay - pulled * normed_learn + content_ref[position] * erasing
        read_ref[position] = jnp.sum(states * acceptor, axis=-1, keepdims=True)


def run_recurrence(starting_memory, vectors, content):
    steps = vectors.shape[0]
    blocks, span, _ = starting_memory.shape
    return pl.pallas_call(
        recurrence_kernel,
        out_shape=jax.ShapeDtypeStruct((steps, blocks, span, 1), jnp.float32),
        in_specs=[pl.BlockSpec(memory_space=pltpu.VMEM)] * 3,
        out_specs=pl.BlockSpec(memory_space=pltpu.VMEM),
    )(starting_memory, vectors, content)


def sequence_recurrence(
    acceptor_entries,
    address_entries,
    content_entries,
    latent_response,
    adapt_latent,
    starting_memory,
    fading_second_lowrank,
    adapt_second_lowrank,
    fading_baseline,
    adapt_baseline,
    erasing_address_gains,
    address_rate_coupling,
    present_extra_gain,
    section_standard_gains,
    section_standard_shift_terms,
):
    batch_rows = starting_memory.shape[0]
    stored_memory_parts = starting_memory.shape[1]
    subspace_span = starting_memory.shape[2]

    def to_heads(array_in):
        return array_in.reshape(batch_rows, -1, stored_memory_parts, subspace_span)

    log_rate = (
        -jax.nn.softplus(
            -(
                fading_baseline
                + jnp.dot(
                    latent_response, fading_second_lowrank, preferred_element_type=jnp.float32
                )
            )
        )
        - 0.5
    )
    decays = to_heads(jnp.exp(-jnp.exp(log_rate)))
    learning = jax.nn.sigmoid(
        adapt_baseline
        + jnp.dot(adapt_latent, adapt_second_lowrank, preferred_element_type=jnp.float32)
    )
    learn_heads = to_heads(learning)
    scaled = to_heads(address_entries * erasing_address_gains)
    normed = scaled / jnp.sqrt(jnp.sum(scaled * scaled, axis=-1, keepdims=True) + 1e-06)
    erasing_flat = address_entries * (1.0 + (learning - 1.0) * address_rate_coupling)
    erasing_address = to_heads(erasing_flat)
    acceptor_parts = to_heads(acceptor_entries)
    content_part_lines = to_heads(content_entries)
    steps_count = acceptor_parts.shape[1]

    def by_step(array_in):
        return jnp.transpose(array_in, (1, 0, 2, 3)).reshape(
            steps_count, batch_rows * stored_memory_parts, 1, subspace_span
        )

    vectors = jnp.stack(
        [
            by_step(decays),
            by_step(normed),
            by_step(normed * learn_heads),
            by_step(erasing_address),
            by_step(acceptor_parts),
        ],
        axis=1,
    )
    content = by_step(content_part_lines).reshape(
        steps_count, batch_rows * stored_memory_parts, subspace_span, 1
    )
    read = run_recurrence(
        starting_memory.reshape(batch_rows * stored_memory_parts, subspace_span, subspace_span),
        vectors,
        content,
    )
    read_all = jnp.transpose(
        read.reshape(steps_count, batch_rows, stored_memory_parts, subspace_span), (1, 0, 2, 3)
    )
    center = read_all - jnp.mean(read_all, axis=-1, keepdims=True)
    variance = jnp.mean(center * center, axis=-1, keepdims=True)
    flat_shape = (batch_rows * acceptor_parts.shape[1], stored_memory_parts * subspace_span)
    standardized_parts = (center / jnp.sqrt(variance + 0.00064)).reshape(
        flat_shape
    ) * section_standard_gains + section_standard_shift_terms
    present_extra_term = (
        jnp.sum(
            to_heads(acceptor_entries * erasing_flat * present_extra_gain),
            axis=-1,
            keepdims=True,
        )
        * content_part_lines
    ).reshape(flat_shape)
    return (standardized_parts + present_extra_term).astype(jnp.bfloat16)


def in_device_order(pieces):
    n = len(pieces)
    me = lax.axis_index("head")
    ordered = []
    for d in range(n):
        chosen = pieces[0]
        for k in range(1, n):
            chosen = jnp.where((me - k) % n == d, pieces[k], chosen)
        ordered.append(chosen)
    return ordered


def gather_heads(block):
    n = lax.axis_size("head")
    pieces = [block]
    for k in range(1, n):
        pieces.append(lax.ppermute(block, "head", [(i, (i + k) % n) for i in range(n)]))
    return in_device_order(pieces)


def scatter_heads(partial):
    n = lax.axis_size("head")
    me = lax.axis_index("head")
    width = partial.shape[1] // n
    total = lax.dynamic_slice_in_dim(partial, me * width, width, 1)
    for k in range(1, n):
        chunk = lax.dynamic_slice_in_dim(partial, ((me + k) % n) * width, width, 1)
        total = total + lax.ppermute(chunk, "head", [(i, (i + k) % n) for i in range(n)])
    return total


def hand_over(partial):
    n = lax.axis_size("head")
    total = None
    for k in range(n):
        piece = lax.ppermute(partial, ("section", "head"), [(i, n + (i + k) % n) for i in range(n)])
        total = piece if total is None else total + piece
    return total


def hand_back(block):
    n = lax.axis_size("head")
    return lax.ppermute(block, ("section", "head"), [(n + i, i) for i in range(n)])


def run_layer(full_now, full_prev_row, params):
    (
        lag_interpolants,
        acceptor_projection,
        address_projection,
        content_projection,
        readout_projection,
        fading_first_full,
        fading_second_lowrank,
        adapt_first_full,
        adapt_second_lowrank,
        fading_baseline,
        adapt_baseline,
        erasing_address_gains,
        address_rate_coupling,
        present_extra_gain,
        section_standard_gains,
        section_standard_shift_terms,
    ) = params
    batch_rows, steps_count, span_width = full_now.shape
    previous = jnp.concatenate([full_prev_row[:, None, :], full_now[:, :-1, :]], axis=1)
    coef_rows = lag_interpolants.astype(jnp.float32)
    current_piece = full_now.astype(jnp.float32)
    spread_piece = previous.astype(jnp.float32) - current_piece
    blends = [
        (current_piece + spread_piece * coef_rows[which_mix])
        .astype(jnp.bfloat16)
        .reshape(-1, span_width)
        for which_mix in range(5)
    ]
    def project(blend, weight):
        return lax.dot_general(
            weight, blend, (((0,), (1,)), ((), ())), preferred_element_type=jnp.float32
        ).T

    acceptor_entries = project(blends[0], acceptor_projection)
    address_entries = project(blends[2], address_projection)
    content_entries = project(blends[3], content_projection)
    latent_response = jnp.tanh(
        jnp.dot(blends[1], fading_first_full, preferred_element_type=jnp.float32)
    ).astype(jnp.bfloat16)
    adapt_latent = jnp.dot(blends[4], adapt_first_full, preferred_element_type=jnp.float32).astype(
        jnp.bfloat16
    )
    return acceptor_entries, address_entries, content_entries, latent_response, adapt_latent


def layer_partial(full_now, full_prev_row, starting_memory, params):
    entries = run_layer(full_now, full_prev_row, params)
    lagged_features = sequence_recurrence(
        *entries,
        starting_memory,
        params[6],
        params[8],
        *params[9:],
    )
    return jnp.dot(lagged_features, params[4], preferred_element_type=jnp.float32)


def run_sections(inputs, states_use, last_use, params):
    section_num = lax.axis_index("section")
    n = lax.axis_size("head")
    batch_rows, steps_count, shard_width = inputs.shape
    fading_first, adapt_first = params[5], params[7]
    sizes = [inputs.size, last_use.size, fading_first.size, adapt_first.size]
    packed = jnp.concatenate(
        [inputs.reshape(-1), last_use.reshape(-1), fading_first.reshape(-1), adapt_first.reshape(-1)]
    )
    ordered = gather_heads(packed)
    cuts = [0]
    for size in sizes:
        cuts.append(cuts[-1] + size)

    def joined(index, shape, axis):
        parts = [piece[cuts[index] : cuts[index + 1]].reshape(shape) for piece in ordered]
        return jnp.concatenate(parts, axis=axis)

    full_first = joined(0, inputs.shape, 2)
    full_prev = joined(1, last_use.shape, 1)
    fading_full = joined(2, fading_first.shape, 0)
    adapt_full = joined(3, adapt_first.shape, 0)
    params = params[:5] + (fading_full, params[6], adapt_full) + params[8:]
    partial_first = layer_partial(full_first, full_prev, states_use, params)
    total_first = hand_over(partial_first)
    full_second = (
        full_first.astype(jnp.float32) + total_first.reshape(full_first.shape)
    ).astype(jnp.bfloat16)
    me = lax.axis_index("head")
    second_in = lax.dynamic_slice_in_dim(full_second, me * shard_width, shard_width, 2)
    first_out = hand_back(second_in)
    partial_second = layer_partial(full_second, full_prev, states_use, params)
    own_second = scatter_heads(partial_second).reshape(batch_rows, steps_count, shard_width)
    second_out = (second_in.astype(jnp.float32) + own_second).astype(jnp.bfloat16)
    return jnp.where(section_num == 0, first_out, second_out)


def body(
    embedding_per_slot,
    tally_per_slot,
    slot_requests,
    memory_per_request,
    previous_step_feature,
    lag_interpolants,
    acceptor_projection,
    address_projection,
    content_projection,
    readout_projection,
    fading_first_lowrank,
    fading_second_lowrank,
    adapt_first_lowrank,
    adapt_second_lowrank,
    fading_baseline,
    adapt_baseline,
    erasing_address_gains,
    address_rate_coupling,
    present_extra_gain,
    section_standard_gains,
    section_standard_shift_terms,
):
    local_rows = embedding_per_slot.shape[0]
    groups = lax.axis_size("req")
    capacity = (local_rows + groups - 1) // groups
    my_group = lax.axis_index("req")
    slot_ids = jnp.arange(local_rows, dtype=jnp.int32)
    table = slot_requests.reshape(groups, local_rows)
    my_arrivals = lax.dynamic_index_in_dim(table, my_group, 0, keepdims=False)
    home_group = my_arrivals // local_rows
    earlier = slot_ids[None, :] < slot_ids[:, None]
    arrival_rank = jnp.sum(
        ((home_group[:, None] == home_group[None, :]) & earlier).astype(jnp.int32), axis=1
    )
    arrival_slot = home_group * capacity + arrival_rank
    requests = my_group * local_rows + slot_ids
    total_rows = slot_requests.shape[0]
    found = slot_requests[None, :] == requests[:, None]
    positions = jnp.sum(
        jnp.where(found, jnp.arange(total_rows, dtype=jnp.int32)[None, :], 0), axis=1
    )
    source = positions // local_rows
    within = positions % local_rows
    source_homes = jnp.take(table, source, axis=0) // local_rows
    home_rank = jnp.sum(
        ((source_homes == my_group) & (slot_ids[None, :] < within[:, None])).astype(jnp.int32),
        axis=1,
    )
    home_slot = source * capacity + home_rank
    buffer_rows = groups * capacity
    params = (
        lag_interpolants.reshape(lag_interpolants.shape[1:]),
        acceptor_projection.reshape(acceptor_projection.shape[1:]),
        address_projection.reshape(address_projection.shape[1:]),
        content_projection.reshape(content_projection.shape[1:]),
        readout_projection.reshape(readout_projection.shape[1:]),
        fading_first_lowrank.reshape(fading_first_lowrank.shape[1:]),
        fading_second_lowrank.reshape(fading_second_lowrank.shape[1:]),
        adapt_first_lowrank.reshape(adapt_first_lowrank.shape[1:]),
        adapt_second_lowrank.reshape(adapt_second_lowrank.shape[1:]),
        fading_baseline,
        adapt_baseline,
        erasing_address_gains,
        address_rate_coupling,
        present_extra_gain,
        section_standard_gains,
        section_standard_shift_terms,
    )
    states_local = memory_per_request.reshape(memory_per_request.shape[1:])
    last_local = previous_step_feature.reshape(previous_step_feature.shape[1:])
    outgoing = (
        jnp.zeros((buffer_rows,) + embedding_per_slot.shape[1:], jnp.bfloat16)
        .at[arrival_slot]
        .set(embedding_per_slot)
    )
    arrived = lax.all_to_all(outgoing, "req", split_axis=0, concat_axis=0, tiled=True)
    inputs = jnp.take(arrived, home_slot, axis=0)
    result = run_sections(inputs, states_local, last_local, params)
    going_back = (
        jnp.zeros((buffer_rows,) + result.shape[1:], jnp.bfloat16).at[home_slot].set(result)
    )
    returned = lax.all_to_all(going_back, "req", split_axis=0, concat_axis=0, tiled=True)
    result = jnp.take(returned, arrival_slot, axis=0)
    live_mask = (
        jnp.arange(embedding_per_slot.shape[1], dtype=jnp.int32)[None, :] < tally_per_slot[:, None]
    )
    return jnp.where(live_mask[:, :, None], result, jnp.zeros_like(result))[None]


def solution(mesh):
    return jax.shard_map(
        body,
        mesh=mesh,
        in_specs=(
            P("req", None, "head"),
            P("req"),
            P(),
            P("section", "req", "head", None, None),
            P("section", "req", "head"),
            P("section", None, None),
            P("section", None, "head"),
            P("section", None, "head"),
            P("section", None, "head"),
            P("section", "head", None),
            P("section", "head", None),
            P("section", None, "head"),
            P("section", "head", None),
            P("section", None, "head"),
            P("section", "head"),
            P("section", "head"),
            P("section", "head"),
            P("section", "head"),
            P("section", "head"),
            P("section", "head"),
            P("section", "head"),
        ),
        out_specs=P("section", "req", None, "head"),
        check_vma=False,
    )
```

```python
import jax
import jax.numpy as jnp
from jax import lax
from jax.experimental import pallas as pl
from jax.experimental.pallas import tpu as pltpu
from jax.sharding import PartitionSpec as P

highest = lax.Precision.HIGHEST


def recurrence_kernel(memory_ref, vector_ref, content_ref, read_ref):
    states = memory_ref[...]
    for position in range(vector_ref.shape[0]):
        decay = vector_ref[position, 0]
        normed = vector_ref[position, 1]
        normed_learn = vector_ref[position, 2]
        erasing = vector_ref[position, 3]
        acceptor = vector_ref[position, 4]
        content = content_ref[position]
        pulled = jnp.sum(states * normed, axis=-1, keepdims=True)
        added = jnp.einsum(
            "bqi,bqj->bij", content, erasing, precision=highest, preferred_element_type=jnp.float32
        )
        states = states * decay - pulled * normed_learn + added
        read_ref[position] = jnp.einsum(
            "bqj,bij->bqi", acceptor, states, precision=highest, preferred_element_type=jnp.float32
        )


def run_recurrence(starting_memory, vectors, content):
    steps = vectors.shape[0]
    blocks, span, _ = starting_memory.shape
    return pl.pallas_call(
        recurrence_kernel,
        out_shape=jax.ShapeDtypeStruct((steps, blocks, 1, span), jnp.float32),
        in_specs=[pl.BlockSpec(memory_space=pltpu.VMEM)] * 3,
        out_specs=pl.BlockSpec(memory_space=pltpu.VMEM),
    )(starting_memory, vectors, content)


def sequence_recurrence(
    acceptor_entries,
    address_entries,
    content_entries,
    latent_response,
    adapt_latent,
    starting_memory,
    fading_second_lowrank,
    adapt_second_lowrank,
    fading_baseline,
    adapt_baseline,
    erasing_address_gains,
    address_rate_coupling,
    present_extra_gain,
    section_standard_gains,
    section_standard_shift_terms,
):
    batch_rows = starting_memory.shape[0]
    stored_memory_parts = starting_memory.shape[1]
    subspace_span = starting_memory.shape[2]

    def to_heads(array_in):
        return array_in.reshape(batch_rows, -1, stored_memory_parts, subspace_span)

    log_rate = (
        -jax.nn.softplus(
            -(
                fading_baseline
                + jnp.dot(
                    latent_response, fading_second_lowrank, preferred_element_type=jnp.float32
                )
            )
        )
        - 0.5
    )
    decays = to_heads(jnp.exp(-jnp.exp(log_rate)))
    learning = jax.nn.sigmoid(
        adapt_baseline
        + jnp.dot(adapt_latent, adapt_second_lowrank, preferred_element_type=jnp.float32)
    )
    learn_heads = to_heads(learning)
    scaled = to_heads(address_entries * erasing_address_gains)
    normed = scaled / jnp.sqrt(jnp.sum(scaled * scaled, axis=-1, keepdims=True) + 1e-06)
    erasing_flat = address_entries * (1.0 + (learning - 1.0) * address_rate_coupling)
    erasing_address = to_heads(erasing_flat)
    acceptor_parts = to_heads(acceptor_entries)
    content_part_lines = to_heads(content_entries)
    steps_count = acceptor_parts.shape[1]

    def by_step(array_in):
        return jnp.transpose(array_in, (1, 0, 2, 3)).reshape(
            steps_count, batch_rows * stored_memory_parts, 1, subspace_span
        )

    vectors = jnp.stack(
        [
            by_step(decays),
            by_step(normed),
            by_step(normed * learn_heads),
            by_step(erasing_address),
            by_step(acceptor_parts),
        ],
        axis=1,
    )
    content = by_step(content_part_lines)
    read = run_recurrence(
        starting_memory.reshape(batch_rows * stored_memory_parts, subspace_span, subspace_span),
        vectors,
        content,
    )
    read_all = jnp.transpose(
        read.reshape(steps_count, batch_rows, stored_memory_parts, subspace_span), (1, 0, 2, 3)
    )
    center = read_all - jnp.mean(read_all, axis=-1, keepdims=True)
    variance = jnp.mean(center * center, axis=-1, keepdims=True)
    flat_shape = (batch_rows * acceptor_parts.shape[1], stored_memory_parts * subspace_span)
    standardized_parts = (center / jnp.sqrt(variance + 0.00064)).reshape(
        flat_shape
    ) * section_standard_gains + section_standard_shift_terms
    present_extra_term = (
        jnp.sum(
            to_heads(acceptor_entries * erasing_flat * present_extra_gain),
            axis=-1,
            keepdims=True,
        )
        * content_part_lines
    ).reshape(flat_shape)
    return (standardized_parts + present_extra_term).astype(jnp.bfloat16)


def in_device_order(pieces):
    n = len(pieces)
    me = lax.axis_index("head")
    ordered = []
    for d in range(n):
        chosen = pieces[0]
        for k in range(1, n):
            chosen = jnp.where((me - k) % n == d, pieces[k], chosen)
        ordered.append(chosen)
    return ordered


def gather_heads(block):
    n = lax.axis_size("head")
    pieces = [block]
    for k in range(1, n):
        pieces.append(lax.ppermute(block, "head", [(i, (i + k) % n) for i in range(n)]))
    return in_device_order(pieces)


def scatter_heads(partial):
    n = lax.axis_size("head")
    me = lax.axis_index("head")
    width = partial.shape[1] // n
    total = lax.dynamic_slice_in_dim(partial, me * width, width, 1)
    for k in range(1, n):
        chunk = lax.dynamic_slice_in_dim(partial, ((me + k) % n) * width, width, 1)
        total = total + lax.ppermute(chunk, "head", [(i, (i + k) % n) for i in range(n)])
    return total


def hand_over(partial):
    n = lax.axis_size("head")
    total = None
    for k in range(n):
        piece = lax.ppermute(partial, ("section", "head"), [(i, n + (i + k) % n) for i in range(n)])
        total = piece if total is None else total + piece
    return total


def hand_back(block):
    n = lax.axis_size("head")
    return lax.ppermute(block, ("section", "head"), [(n + i, i) for i in range(n)])


def run_layer(full_now, full_prev_row, params):
    (
        lag_interpolants,
        acceptor_projection,
        address_projection,
        content_projection,
        readout_projection,
        fading_first_full,
        fading_second_lowrank,
        adapt_first_full,
        adapt_second_lowrank,
        fading_baseline,
        adapt_baseline,
        erasing_address_gains,
        address_rate_coupling,
        present_extra_gain,
        section_standard_gains,
        section_standard_shift_terms,
    ) = params
    batch_rows, steps_count, span_width = full_now.shape
    previous = jnp.concatenate([full_prev_row[:, None, :], full_now[:, :-1, :]], axis=1)
    coef_rows = lag_interpolants.astype(jnp.float32)
    current_piece = full_now.astype(jnp.float32)
    spread_piece = previous.astype(jnp.float32) - current_piece
    blends = [
        (current_piece + spread_piece * coef_rows[which_mix])
        .astype(jnp.bfloat16)
        .reshape(-1, span_width)
        for which_mix in range(5)
    ]
    def project(blend, weight):
        return lax.dot_general(
            weight, blend, (((0,), (1,)), ((), ())), preferred_element_type=jnp.float32
        ).T

    acceptor_entries = project(blends[0], acceptor_projection)
    address_entries = project(blends[2], address_projection)
    content_entries = project(blends[3], content_projection)
    latent_response = jnp.tanh(
        jnp.dot(blends[1], fading_first_full, preferred_element_type=jnp.float32)
    ).astype(jnp.bfloat16)
    adapt_latent = jnp.dot(blends[4], adapt_first_full, preferred_element_type=jnp.float32).astype(
        jnp.bfloat16
    )
    return acceptor_entries, address_entries, content_entries, latent_response, adapt_latent


def layer_partial(full_now, full_prev_row, starting_memory, params):
    entries = run_layer(full_now, full_prev_row, params)
    lagged_features = sequence_recurrence(
        *entries,
        starting_memory,
        params[6],
        params[8],
        *params[9:],
    )
    return jnp.dot(lagged_features, params[4], preferred_element_type=jnp.float32)


def run_sections(inputs, states_use, last_use, params):
    section_num = lax.axis_index("section")
    n = lax.axis_size("head")
    batch_rows, steps_count, shard_width = inputs.shape
    fading_first, adapt_first = params[5], params[7]
    sizes = [inputs.size, last_use.size, fading_first.size, adapt_first.size]
    packed = jnp.concatenate(
        [inputs.reshape(-1), last_use.reshape(-1), fading_first.reshape(-1), adapt_first.reshape(-1)]
    )
    ordered = gather_heads(packed)
    cuts = [0]
    for size in sizes:
        cuts.append(cuts[-1] + size)

    def joined(index, shape, axis):
        parts = [piece[cuts[index] : cuts[index + 1]].reshape(shape) for piece in ordered]
        return jnp.concatenate(parts, axis=axis)

    full_first = joined(0, inputs.shape, 2)
    full_prev = joined(1, last_use.shape, 1)
    fading_full = joined(2, fading_first.shape, 0)
    adapt_full = joined(3, adapt_first.shape, 0)
    params = params[:5] + (fading_full, params[6], adapt_full) + params[8:]
    partial_first = layer_partial(full_first, full_prev, states_use, params)
    total_first = hand_over(partial_first)
    full_second = (
        full_first.astype(jnp.float32) + total_first.reshape(full_first.shape)
    ).astype(jnp.bfloat16)
    me = lax.axis_index("head")
    second_in = lax.dynamic_slice_in_dim(full_second, me * shard_width, shard_width, 2)
    first_out = hand_back(second_in)
    partial_second = layer_partial(full_second, full_prev, states_use, params)
    own_second = scatter_heads(partial_second).reshape(batch_rows, steps_count, shard_width)
    second_out = (second_in.astype(jnp.float32) + own_second).astype(jnp.bfloat16)
    return jnp.where(section_num == 0, first_out, second_out)


def body(
    embedding_per_slot,
    tally_per_slot,
    slot_requests,
    memory_per_request,
    previous_step_feature,
    lag_interpolants,
    acceptor_projection,
    address_projection,
    content_projection,
    readout_projection,
    fading_first_lowrank,
    fading_second_lowrank,
    adapt_first_lowrank,
    adapt_second_lowrank,
    fading_baseline,
    adapt_baseline,
    erasing_address_gains,
    address_rate_coupling,
    present_extra_gain,
    section_standard_gains,
    section_standard_shift_terms,
):
    local_rows = embedding_per_slot.shape[0]
    groups = lax.axis_size("req")
    capacity = (local_rows + groups - 1) // groups
    my_group = lax.axis_index("req")
    slot_ids = jnp.arange(local_rows, dtype=jnp.int32)
    table = slot_requests.reshape(groups, local_rows)
    my_arrivals = lax.dynamic_index_in_dim(table, my_group, 0, keepdims=False)
    home_group = my_arrivals // local_rows
    earlier = slot_ids[None, :] < slot_ids[:, None]
    arrival_rank = jnp.sum(
        ((home_group[:, None] == home_group[None, :]) & earlier).astype(jnp.int32), axis=1
    )
    arrival_slot = home_group * capacity + arrival_rank
    requests = my_group * local_rows + slot_ids
    total_rows = slot_requests.shape[0]
    found = slot_requests[None, :] == requests[:, None]
    positions = jnp.sum(
        jnp.where(found, jnp.arange(total_rows, dtype=jnp.int32)[None, :], 0), axis=1
    )
    source = positions // local_rows
    within = positions % local_rows
    source_homes = jnp.take(table, source, axis=0) // local_rows
    home_rank = jnp.sum(
        ((source_homes == my_group) & (slot_ids[None, :] < within[:, None])).astype(jnp.int32),
        axis=1,
    )
    home_slot = source * capacity + home_rank
    buffer_rows = groups * capacity
    params = (
        lag_interpolants.reshape(lag_interpolants.shape[1:]),
        acceptor_projection.reshape(acceptor_projection.shape[1:]),
        address_projection.reshape(address_projection.shape[1:]),
        content_projection.reshape(content_projection.shape[1:]),
        readout_projection.reshape(readout_projection.shape[1:]),
        fading_first_lowrank.reshape(fading_first_lowrank.shape[1:]),
        fading_second_lowrank.reshape(fading_second_lowrank.shape[1:]),
        adapt_first_lowrank.reshape(adapt_first_lowrank.shape[1:]),
        adapt_second_lowrank.reshape(adapt_second_lowrank.shape[1:]),
        fading_baseline,
        adapt_baseline,
        erasing_address_gains,
        address_rate_coupling,
        present_extra_gain,
        section_standard_gains,
        section_standard_shift_terms,
    )
    states_local = memory_per_request.reshape(memory_per_request.shape[1:])
    last_local = previous_step_feature.reshape(previous_step_feature.shape[1:])
    outgoing = (
        jnp.zeros((buffer_rows,) + embedding_per_slot.shape[1:], jnp.bfloat16)
        .at[arrival_slot]
        .set(embedding_per_slot)
    )
    arrived = lax.all_to_all(outgoing, "req", split_axis=0, concat_axis=0, tiled=True)
    inputs = jnp.take(arrived, home_slot, axis=0)
    result = run_sections(inputs, states_local, last_local, params)
    going_back = (
        jnp.zeros((buffer_rows,) + result.shape[1:], jnp.bfloat16).at[home_slot].set(result)
    )
    returned = lax.all_to_all(going_back, "req", split_axis=0, concat_axis=0, tiled=True)
    result = jnp.take(returned, arrival_slot, axis=0)
    live_mask = (
        jnp.arange(embedding_per_slot.shape[1], dtype=jnp.int32)[None, :] < tally_per_slot[:, None]
    )
    return jnp.where(live_mask[:, :, None], result, jnp.zeros_like(result))[None]


def solution(mesh):
    return jax.shard_map(
        body,
        mesh=mesh,
        in_specs=(
            P("req", None, "head"),
            P("req"),
            P(),
            P("section", "req", "head", None, None),
            P("section", "req", "head"),
            P("section", None, None),
            P("section", None, "head"),
            P("section", None, "head"),
            P("section", None, "head"),
            P("section", "head", None),
            P("section", "head", None),
            P("section", None, "head"),
            P("section", "head", None),
            P("section", None, "head"),
            P("section", "head"),
            P("section", "head"),
            P("section", "head"),
            P("section", "head"),
            P("section", "head"),
            P("section", "head"),
            P("section", "head"),
        ),
        out_specs=P("section", "req", None, "head"),
        check_vma=False,
    )
```

```python
import jax
import jax.numpy as jnp
from jax import lax
from jax.experimental import pallas as pl
from jax.experimental.pallas import tpu as pltpu
from jax.sharding import PartitionSpec as P

highest = lax.Precision.HIGHEST


def recurrence_kernel(memory_ref, vector_ref, content_ref, read_ref):
    states = memory_ref[...]
    for position in range(vector_ref.shape[0]):
        decay = vector_ref[position, 0]
        normed = vector_ref[position, 1]
        normed_learn = vector_ref[position, 2]
        erasing = vector_ref[position, 3]
        acceptor = vector_ref[position, 4]
        content = content_ref[position]
        pulled = jnp.sum(states * normed, axis=-1, keepdims=True)
        added = jnp.einsum(
            "bqi,bqj->bij", content, erasing, precision=lax.Precision.HIGH, preferred_element_type=jnp.float32
        )
        states = states * decay - pulled * normed_learn + added
        read_ref[position] = jnp.einsum(
            "bqj,bij->bqi", acceptor, states, precision=lax.Precision.HIGH, preferred_element_type=jnp.float32
        )


def run_recurrence(starting_memory, vectors, content):
    steps = vectors.shape[0]
    blocks, span, _ = starting_memory.shape
    return pl.pallas_call(
        recurrence_kernel,
        out_shape=jax.ShapeDtypeStruct((steps, blocks, 1, span), jnp.float32),
        in_specs=[pl.BlockSpec(memory_space=pltpu.VMEM)] * 3,
        out_specs=pl.BlockSpec(memory_space=pltpu.VMEM),
    )(starting_memory, vectors, content)


def sequence_recurrence(
    acceptor_entries,
    address_entries,
    content_entries,
    latent_response,
    adapt_latent,
    starting_memory,
    fading_second_lowrank,
    adapt_second_lowrank,
    fading_baseline,
    adapt_baseline,
    erasing_address_gains,
    address_rate_coupling,
    present_extra_gain,
    section_standard_gains,
    section_standard_shift_terms,
):
    batch_rows = starting_memory.shape[0]
    stored_memory_parts = starting_memory.shape[1]
    subspace_span = starting_memory.shape[2]

    def to_heads(array_in):
        return array_in.reshape(batch_rows, -1, stored_memory_parts, subspace_span)

    log_rate = (
        -jax.nn.softplus(
            -(
                fading_baseline
                + jnp.dot(
                    latent_response, fading_second_lowrank, preferred_element_type=jnp.float32
                )
            )
        )
        - 0.5
    )
    decays = to_heads(jnp.exp(-jnp.exp(log_rate)))
    learning = jax.nn.sigmoid(
        adapt_baseline
        + jnp.dot(adapt_latent, adapt_second_lowrank, preferred_element_type=jnp.float32)
    )
    learn_heads = to_heads(learning)
    scaled = to_heads(address_entries * erasing_address_gains)
    normed = scaled / jnp.sqrt(jnp.sum(scaled * scaled, axis=-1, keepdims=True) + 1e-06)
    erasing_flat = address_entries * (1.0 + (learning - 1.0) * address_rate_coupling)
    erasing_address = to_heads(erasing_flat)
    acceptor_parts = to_heads(acceptor_entries)
    content_part_lines = to_heads(content_entries)
    steps_count = acceptor_parts.shape[1]

    def by_step(array_in):
        return jnp.transpose(array_in, (1, 0, 2, 3)).reshape(
            steps_count, batch_rows * stored_memory_parts, 1, subspace_span
        )

    vectors = jnp.stack(
        [
            by_step(decays),
            by_step(normed),
            by_step(normed * learn_heads),
            by_step(erasing_address),
            by_step(acceptor_parts),
        ],
        axis=1,
    )
    content = by_step(content_part_lines)
    read = run_recurrence(
        starting_memory.reshape(batch_rows * stored_memory_parts, subspace_span, subspace_span),
        vectors,
        content,
    )
    read_all = jnp.transpose(
        read.reshape(steps_count, batch_rows, stored_memory_parts, subspace_span), (1, 0, 2, 3)
    )
    center = read_all - jnp.mean(read_all, axis=-1, keepdims=True)
    variance = jnp.mean(center * center, axis=-1, keepdims=True)
    flat_shape = (batch_rows * acceptor_parts.shape[1], stored_memory_parts * subspace_span)
    standardized_parts = (center / jnp.sqrt(variance + 0.00064)).reshape(
        flat_shape
    ) * section_standard_gains + section_standard_shift_terms
    present_extra_term = (
        jnp.sum(
            to_heads(acceptor_entries * erasing_flat * present_extra_gain),
            axis=-1,
            keepdims=True,
        )
        * content_part_lines
    ).reshape(flat_shape)
    return (standardized_parts + present_extra_term).astype(jnp.bfloat16)


def in_device_order(pieces):
    n = len(pieces)
    me = lax.axis_index("head")
    ordered = []
    for d in range(n):
        chosen = pieces[0]
        for k in range(1, n):
            chosen = jnp.where((me - k) % n == d, pieces[k], chosen)
        ordered.append(chosen)
    return ordered


def gather_heads(block):
    n = lax.axis_size("head")
    pieces = [block]
    for k in range(1, n):
        pieces.append(lax.ppermute(block, "head", [(i, (i + k) % n) for i in range(n)]))
    return in_device_order(pieces)


def scatter_heads(partial):
    n = lax.axis_size("head")
    me = lax.axis_index("head")
    width = partial.shape[1] // n
    total = lax.dynamic_slice_in_dim(partial, me * width, width, 1)
    for k in range(1, n):
        chunk = lax.dynamic_slice_in_dim(partial, ((me + k) % n) * width, width, 1)
        total = total + lax.ppermute(chunk, "head", [(i, (i + k) % n) for i in range(n)])
    return total


def hand_over(partial):
    n = lax.axis_size("head")
    total = None
    for k in range(n):
        piece = lax.ppermute(partial, ("section", "head"), [(i, n + (i + k) % n) for i in range(n)])
        total = piece if total is None else total + piece
    return total


def hand_back(block):
    n = lax.axis_size("head")
    return lax.ppermute(block, ("section", "head"), [(n + i, i) for i in range(n)])


def run_layer(full_now, full_prev_row, params):
    (
        lag_interpolants,
        acceptor_projection,
        address_projection,
        content_projection,
        readout_projection,
        fading_first_full,
        fading_second_lowrank,
        adapt_first_full,
        adapt_second_lowrank,
        fading_baseline,
        adapt_baseline,
        erasing_address_gains,
        address_rate_coupling,
        present_extra_gain,
        section_standard_gains,
        section_standard_shift_terms,
    ) = params
    batch_rows, steps_count, span_width = full_now.shape
    previous = jnp.concatenate([full_prev_row[:, None, :], full_now[:, :-1, :]], axis=1)
    coef_rows = lag_interpolants.astype(jnp.float32)
    current_piece = full_now.astype(jnp.float32)
    spread_piece = previous.astype(jnp.float32) - current_piece
    blends = [
        (current_piece + spread_piece * coef_rows[which_mix])
        .astype(jnp.bfloat16)
        .reshape(-1, span_width)
        for which_mix in range(5)
    ]
    def project(blend, weight):
        return lax.dot_general(
            weight, blend, (((0,), (1,)), ((), ())), preferred_element_type=jnp.float32
        ).T

    acceptor_entries = project(blends[0], acceptor_projection)
    address_entries = project(blends[2], address_projection)
    content_entries = project(blends[3], content_projection)
    latent_response = jnp.tanh(
        jnp.dot(blends[1], fading_first_full, preferred_element_type=jnp.float32)
    ).astype(jnp.bfloat16)
    adapt_latent = jnp.dot(blends[4], adapt_first_full, preferred_element_type=jnp.float32).astype(
        jnp.bfloat16
    )
    return acceptor_entries, address_entries, content_entries, latent_response, adapt_latent


def layer_partial(full_now, full_prev_row, starting_memory, params):
    entries = run_layer(full_now, full_prev_row, params)
    lagged_features = sequence_recurrence(
        *entries,
        starting_memory,
        params[6],
        params[8],
        *params[9:],
    )
    return jnp.dot(lagged_features, params[4], preferred_element_type=jnp.float32)


def run_sections(inputs, states_use, last_use, params):
    section_num = lax.axis_index("section")
    n = lax.axis_size("head")
    batch_rows, steps_count, shard_width = inputs.shape
    fading_first, adapt_first = params[5], params[7]
    sizes = [inputs.size, last_use.size, fading_first.size, adapt_first.size]
    packed = jnp.concatenate(
        [inputs.reshape(-1), last_use.reshape(-1), fading_first.reshape(-1), adapt_first.reshape(-1)]
    )
    ordered = gather_heads(packed)
    cuts = [0]
    for size in sizes:
        cuts.append(cuts[-1] + size)

    def joined(index, shape, axis):
        parts = [piece[cuts[index] : cuts[index + 1]].reshape(shape) for piece in ordered]
        return jnp.concatenate(parts, axis=axis)

    full_first = joined(0, inputs.shape, 2)
    full_prev = joined(1, last_use.shape, 1)
    fading_full = joined(2, fading_first.shape, 0)
    adapt_full = joined(3, adapt_first.shape, 0)
    params = params[:5] + (fading_full, params[6], adapt_full) + params[8:]
    partial_first = layer_partial(full_first, full_prev, states_use, params)
    total_first = hand_over(partial_first)
    full_second = (
        full_first.astype(jnp.float32) + total_first.reshape(full_first.shape)
    ).astype(jnp.bfloat16)
    me = lax.axis_index("head")
    second_in = lax.dynamic_slice_in_dim(full_second, me * shard_width, shard_width, 2)
    first_out = hand_back(second_in)
    partial_second = layer_partial(full_second, full_prev, states_use, params)
    own_second = scatter_heads(partial_second).reshape(batch_rows, steps_count, shard_width)
    second_out = (second_in.astype(jnp.float32) + own_second).astype(jnp.bfloat16)
    return jnp.where(section_num == 0, first_out, second_out)


def body(
    embedding_per_slot,
    tally_per_slot,
    slot_requests,
    memory_per_request,
    previous_step_feature,
    lag_interpolants,
    acceptor_projection,
    address_projection,
    content_projection,
    readout_projection,
    fading_first_lowrank,
    fading_second_lowrank,
    adapt_first_lowrank,
    adapt_second_lowrank,
    fading_baseline,
    adapt_baseline,
    erasing_address_gains,
    address_rate_coupling,
    present_extra_gain,
    section_standard_gains,
    section_standard_shift_terms,
):
    local_rows = embedding_per_slot.shape[0]
    groups = lax.axis_size("req")
    capacity = (local_rows + groups - 1) // groups
    my_group = lax.axis_index("req")
    slot_ids = jnp.arange(local_rows, dtype=jnp.int32)
    table = slot_requests.reshape(groups, local_rows)
    my_arrivals = lax.dynamic_index_in_dim(table, my_group, 0, keepdims=False)
    home_group = my_arrivals // local_rows
    earlier = slot_ids[None, :] < slot_ids[:, None]
    arrival_rank = jnp.sum(
        ((home_group[:, None] == home_group[None, :]) & earlier).astype(jnp.int32), axis=1
    )
    arrival_slot = home_group * capacity + arrival_rank
    requests = my_group * local_rows + slot_ids
    total_rows = slot_requests.shape[0]
    found = slot_requests[None, :] == requests[:, None]
    positions = jnp.sum(
        jnp.where(found, jnp.arange(total_rows, dtype=jnp.int32)[None, :], 0), axis=1
    )
    source = positions // local_rows
    within = positions % local_rows
    source_homes = jnp.take(table, source, axis=0) // local_rows
    home_rank = jnp.sum(
        ((source_homes == my_group) & (slot_ids[None, :] < within[:, None])).astype(jnp.int32),
        axis=1,
    )
    home_slot = source * capacity + home_rank
    buffer_rows = groups * capacity
    params = (
        lag_interpolants.reshape(lag_interpolants.shape[1:]),
        acceptor_projection.reshape(acceptor_projection.shape[1:]),
        address_projection.reshape(address_projection.shape[1:]),
        content_projection.reshape(content_projection.shape[1:]),
        readout_projection.reshape(readout_projection.shape[1:]),
        fading_first_lowrank.reshape(fading_first_lowrank.shape[1:]),
        fading_second_lowrank.reshape(fading_second_lowrank.shape[1:]),
        adapt_first_lowrank.reshape(adapt_first_lowrank.shape[1:]),
        adapt_second_lowrank.reshape(adapt_second_lowrank.shape[1:]),
        fading_baseline,
        adapt_baseline,
        erasing_address_gains,
        address_rate_coupling,
        present_extra_gain,
        section_standard_gains,
        section_standard_shift_terms,
    )
    states_local = memory_per_request.reshape(memory_per_request.shape[1:])
    last_local = previous_step_feature.reshape(previous_step_feature.shape[1:])
    outgoing = (
        jnp.zeros((buffer_rows,) + embedding_per_slot.shape[1:], jnp.bfloat16)
        .at[arrival_slot]
        .set(embedding_per_slot)
    )
    arrived = lax.all_to_all(outgoing, "req", split_axis=0, concat_axis=0, tiled=True)
    inputs = jnp.take(arrived, home_slot, axis=0)
    result = run_sections(inputs, states_local, last_local, params)
    going_back = (
        jnp.zeros((buffer_rows,) + result.shape[1:], jnp.bfloat16).at[home_slot].set(result)
    )
    returned = lax.all_to_all(going_back, "req", split_axis=0, concat_axis=0, tiled=True)
    result = jnp.take(returned, arrival_slot, axis=0)
    live_mask = (
        jnp.arange(embedding_per_slot.shape[1], dtype=jnp.int32)[None, :] < tally_per_slot[:, None]
    )
    return jnp.where(live_mask[:, :, None], result, jnp.zeros_like(result))[None]


def solution(mesh):
    return jax.shard_map(
        body,
        mesh=mesh,
        in_specs=(
            P("req", None, "head"),
            P("req"),
            P(),
            P("section", "req", "head", None, None),
            P("section", "req", "head"),
            P("section", None, None),
            P("section", None, "head"),
            P("section", None, "head"),
            P("section", None, "head"),
            P("section", "head", None),
            P("section", "head", None),
            P("section", None, "head"),
            P("section", "head", None),
            P("section", None, "head"),
            P("section", "head"),
            P("section", "head"),
            P("section", "head"),
            P("section", "head"),
            P("section", "head"),
            P("section", "head"),
            P("section", "head"),
        ),
        out_specs=P("section", "req", None, "head"),
        check_vma=False,
    )
```

```python
import jax
import jax.numpy as jnp
from jax import lax
from jax.experimental import pallas as pl
from jax.experimental.pallas import tpu as pltpu
from jax.sharding import PartitionSpec as P

highest = lax.Precision.HIGHEST


def recurrence_kernel(memory_ref, vector_ref, content_ref, read_ref):
    states = memory_ref[...]
    for position in range(vector_ref.shape[0]):
        decay = vector_ref[position, 0]
        normed = vector_ref[position, 1]
        normed_learn = vector_ref[position, 2]
        erasing = vector_ref[position, 3]
        acceptor = vector_ref[position, 4]
        content = content_ref[position]
        pulled = jnp.sum(states * normed, axis=-1, keepdims=True)
        added = jnp.einsum(
            "bqi,bqj->bij", content, erasing, precision=lax.Precision.HIGH, preferred_element_type=jnp.float32
        )
        states = states * decay - pulled * normed_learn + added
        read_ref[position] = jnp.einsum(
            "bqj,bij->bqi", acceptor, states, precision=lax.Precision.HIGH, preferred_element_type=jnp.float32
        )


def run_recurrence(starting_memory, vectors, content):
    steps = vectors.shape[0]
    blocks, span, _ = starting_memory.shape
    return pl.pallas_call(
        recurrence_kernel,
        out_shape=jax.ShapeDtypeStruct((steps, blocks, 1, span), jnp.float32),
        in_specs=[pl.BlockSpec(memory_space=pltpu.VMEM)] * 3,
        out_specs=pl.BlockSpec(memory_space=pltpu.VMEM),
    )(starting_memory, vectors, content)


def sequence_recurrence(
    acceptor_entries,
    address_entries,
    content_entries,
    latent_response,
    adapt_latent,
    starting_memory,
    fading_second_lowrank,
    adapt_second_lowrank,
    fading_baseline,
    adapt_baseline,
    erasing_address_gains,
    address_rate_coupling,
    present_extra_gain,
    section_standard_gains,
    section_standard_shift_terms,
):
    batch_rows = starting_memory.shape[0]
    stored_memory_parts = starting_memory.shape[1]
    subspace_span = starting_memory.shape[2]

    def to_heads(array_in):
        return array_in.reshape(batch_rows, -1, stored_memory_parts, subspace_span)

    log_rate = (
        -jax.nn.softplus(
            -(
                fading_baseline
                + jnp.dot(
                    latent_response, fading_second_lowrank, preferred_element_type=jnp.float32
                )
            )
        )
        - 0.5
    )
    decays = to_heads(jnp.exp(-jnp.exp(log_rate)))
    learning = jax.nn.sigmoid(
        adapt_baseline
        + jnp.dot(adapt_latent, adapt_second_lowrank, preferred_element_type=jnp.float32)
    )
    learn_heads = to_heads(learning)
    scaled = to_heads(address_entries * erasing_address_gains)
    normed = scaled / jnp.sqrt(jnp.sum(scaled * scaled, axis=-1, keepdims=True) + 1e-06)
    erasing_flat = address_entries * (1.0 + (learning - 1.0) * address_rate_coupling)
    erasing_address = to_heads(erasing_flat)
    acceptor_parts = to_heads(acceptor_entries)
    content_part_lines = to_heads(content_entries)
    steps_count = acceptor_parts.shape[1]

    def by_step(array_in):
        return jnp.transpose(array_in, (1, 0, 2, 3)).reshape(
            steps_count, batch_rows * stored_memory_parts, 1, subspace_span
        )

    vectors = jnp.stack(
        [
            by_step(decays),
            by_step(normed),
            by_step(normed * learn_heads),
            by_step(erasing_address),
            by_step(acceptor_parts),
        ],
        axis=1,
    )
    content = by_step(content_part_lines)
    read = run_recurrence(
        starting_memory.reshape(batch_rows * stored_memory_parts, subspace_span, subspace_span),
        vectors,
        content,
    )
    read_all = jnp.transpose(
        read.reshape(steps_count, batch_rows, stored_memory_parts, subspace_span), (1, 0, 2, 3)
    )
    center = read_all - jnp.mean(read_all, axis=-1, keepdims=True)
    variance = jnp.mean(center * center, axis=-1, keepdims=True)
    flat_shape = (batch_rows * acceptor_parts.shape[1], stored_memory_parts * subspace_span)
    standardized_parts = (center / jnp.sqrt(variance + 0.00064)).reshape(
        flat_shape
    ) * section_standard_gains + section_standard_shift_terms
    present_extra_term = (
        jnp.sum(
            to_heads(acceptor_entries * erasing_flat * present_extra_gain),
            axis=-1,
            keepdims=True,
        )
        * content_part_lines
    ).reshape(flat_shape)
    return (standardized_parts + present_extra_term).astype(jnp.bfloat16)


def in_device_order(pieces):
    n = len(pieces)
    me = lax.axis_index("head")
    ordered = []
    for d in range(n):
        chosen = pieces[0]
        for k in range(1, n):
            chosen = jnp.where((me - k) % n == d, pieces[k], chosen)
        ordered.append(chosen)
    return ordered


def gather_heads(block):
    n = lax.axis_size("head")
    pieces = [block]
    for k in range(1, n):
        pieces.append(lax.ppermute(block, "head", [(i, (i + k) % n) for i in range(n)]))
    return in_device_order(pieces)


def scatter_heads(partial):
    n = lax.axis_size("head")
    me = lax.axis_index("head")
    width = partial.shape[1] // n
    total = lax.dynamic_slice_in_dim(partial, me * width, width, 1)
    for k in range(1, n):
        chunk = lax.dynamic_slice_in_dim(partial, ((me + k) % n) * width, width, 1)
        total = total + lax.ppermute(chunk, "head", [(i, (i + k) % n) for i in range(n)])
    return total


def hand_over(partial):
    n = lax.axis_size("head")
    total = None
    for k in range(n):
        piece = lax.ppermute(partial, ("section", "head"), [(i, n + (i + k) % n) for i in range(n)])
        total = piece if total is None else total + piece
    return total


def hand_back(block):
    n = lax.axis_size("head")
    return lax.ppermute(block, ("section", "head"), [(n + i, i) for i in range(n)])


def run_layer(full_now, full_prev_row, params):
    (
        lag_interpolants,
        acceptor_projection,
        address_projection,
        content_projection,
        readout_projection,
        fading_first_full,
        fading_second_lowrank,
        adapt_first_full,
        adapt_second_lowrank,
        fading_baseline,
        adapt_baseline,
        erasing_address_gains,
        address_rate_coupling,
        present_extra_gain,
        section_standard_gains,
        section_standard_shift_terms,
    ) = params
    batch_rows, steps_count, span_width = full_now.shape
    previous = jnp.concatenate([full_prev_row[:, None, :], full_now[:, :-1, :]], axis=1)
    coef_rows = lag_interpolants.astype(jnp.float32)
    current_piece = full_now.astype(jnp.float32)
    spread_piece = previous.astype(jnp.float32) - current_piece
    blends = [
        (current_piece + spread_piece * coef_rows[which_mix])
        .astype(jnp.bfloat16)
        .reshape(-1, span_width)
        for which_mix in range(5)
    ]
    def project(blend, weight):
        return lax.dot_general(
            weight, blend, (((0,), (1,)), ((), ())), preferred_element_type=jnp.float32
        ).T

    acceptor_entries = project(blends[0], acceptor_projection)
    address_entries = project(blends[2], address_projection)
    content_entries = project(blends[3], content_projection)
    latent_response = jnp.tanh(
        jnp.dot(blends[1], fading_first_full, preferred_element_type=jnp.float32)
    ).astype(jnp.bfloat16)
    adapt_latent = jnp.dot(blends[4], adapt_first_full, preferred_element_type=jnp.float32).astype(
        jnp.bfloat16
    )
    return acceptor_entries, address_entries, content_entries, latent_response, adapt_latent


def layer_partial(full_now, full_prev_row, starting_memory, params):
    entries = run_layer(full_now, full_prev_row, params)
    lagged_features = sequence_recurrence(
        *entries,
        starting_memory,
        params[6],
        params[8],
        *params[9:],
    )
    return jnp.dot(lagged_features, params[4], preferred_element_type=jnp.float32)


def run_sections(inputs, states_use, last_use, params):
    section_num = lax.axis_index("section")
    n = lax.axis_size("head")
    batch_rows, steps_count, shard_width = inputs.shape
    fading_first, adapt_first = params[5], params[7]
    sizes = [inputs.size, last_use.size, fading_first.size, adapt_first.size]
    packed = jnp.concatenate(
        [inputs.reshape(-1), last_use.reshape(-1), fading_first.reshape(-1), adapt_first.reshape(-1)]
    )
    ordered = gather_heads(packed)
    cuts = [0]
    for size in sizes:
        cuts.append(cuts[-1] + size)

    def joined(index, shape, axis):
        parts = [piece[cuts[index] : cuts[index + 1]].reshape(shape) for piece in ordered]
        return jnp.concatenate(parts, axis=axis)

    full_first = joined(0, inputs.shape, 2)
    full_prev = joined(1, last_use.shape, 1)
    fading_full = joined(2, fading_first.shape, 0)
    adapt_full = joined(3, adapt_first.shape, 0)
    params = params[:5] + (fading_full, params[6], adapt_full) + params[8:]
    partial_first = layer_partial(full_first, full_prev, states_use, params)
    total_first = hand_over(partial_first)
    full_second = (
        full_first.astype(jnp.float32) + total_first.reshape(full_first.shape)
    ).astype(jnp.bfloat16)
    me = lax.axis_index("head")
    second_in = lax.dynamic_slice_in_dim(full_second, me * shard_width, shard_width, 2)
    first_out = lax.cond(
        section_num == 0,
        lambda part: (
            inputs.astype(jnp.float32)
            + scatter_heads(part).reshape(batch_rows, steps_count, shard_width)
        ).astype(jnp.bfloat16),
        lambda part: jnp.zeros_like(inputs),
        partial_first,
    )
    partial_second = layer_partial(full_second, full_prev, states_use, params)
    own_second = scatter_heads(partial_second).reshape(batch_rows, steps_count, shard_width)
    second_out = (second_in.astype(jnp.float32) + own_second).astype(jnp.bfloat16)
    return jnp.where(section_num == 0, first_out, second_out)


def body(
    embedding_per_slot,
    tally_per_slot,
    slot_requests,
    memory_per_request,
    previous_step_feature,
    lag_interpolants,
    acceptor_projection,
    address_projection,
    content_projection,
    readout_projection,
    fading_first_lowrank,
    fading_second_lowrank,
    adapt_first_lowrank,
    adapt_second_lowrank,
    fading_baseline,
    adapt_baseline,
    erasing_address_gains,
    address_rate_coupling,
    present_extra_gain,
    section_standard_gains,
    section_standard_shift_terms,
):
    local_rows = embedding_per_slot.shape[0]
    groups = lax.axis_size("req")
    capacity = (local_rows + groups - 1) // groups
    my_group = lax.axis_index("req")
    slot_ids = jnp.arange(local_rows, dtype=jnp.int32)
    table = slot_requests.reshape(groups, local_rows)
    my_arrivals = lax.dynamic_index_in_dim(table, my_group, 0, keepdims=False)
    home_group = my_arrivals // local_rows
    earlier = slot_ids[None, :] < slot_ids[:, None]
    arrival_rank = jnp.sum(
        ((home_group[:, None] == home_group[None, :]) & earlier).astype(jnp.int32), axis=1
    )
    arrival_slot = home_group * capacity + arrival_rank
    requests = my_group * local_rows + slot_ids
    total_rows = slot_requests.shape[0]
    found = slot_requests[None, :] == requests[:, None]
    positions = jnp.sum(
        jnp.where(found, jnp.arange(total_rows, dtype=jnp.int32)[None, :], 0), axis=1
    )
    source = positions // local_rows
    within = positions % local_rows
    source_homes = jnp.take(table, source, axis=0) // local_rows
    home_rank = jnp.sum(
        ((source_homes == my_group) & (slot_ids[None, :] < within[:, None])).astype(jnp.int32),
        axis=1,
    )
    home_slot = source * capacity + home_rank
    buffer_rows = groups * capacity
    params = (
        lag_interpolants.reshape(lag_interpolants.shape[1:]),
        acceptor_projection.reshape(acceptor_projection.shape[1:]),
        address_projection.reshape(address_projection.shape[1:]),
        content_projection.reshape(content_projection.shape[1:]),
        readout_projection.reshape(readout_projection.shape[1:]),
        fading_first_lowrank.reshape(fading_first_lowrank.shape[1:]),
        fading_second_lowrank.reshape(fading_second_lowrank.shape[1:]),
        adapt_first_lowrank.reshape(adapt_first_lowrank.shape[1:]),
        adapt_second_lowrank.reshape(adapt_second_lowrank.shape[1:]),
        fading_baseline,
        adapt_baseline,
        erasing_address_gains,
        address_rate_coupling,
        present_extra_gain,
        section_standard_gains,
        section_standard_shift_terms,
    )
    states_local = memory_per_request.reshape(memory_per_request.shape[1:])
    last_local = previous_step_feature.reshape(previous_step_feature.shape[1:])
    outgoing = (
        jnp.zeros((buffer_rows,) + embedding_per_slot.shape[1:], jnp.bfloat16)
        .at[arrival_slot]
        .set(embedding_per_slot)
    )
    arrived = lax.all_to_all(outgoing, "req", split_axis=0, concat_axis=0, tiled=True)
    inputs = jnp.take(arrived, home_slot, axis=0)
    result = run_sections(inputs, states_local, last_local, params)
    going_back = (
        jnp.zeros((buffer_rows,) + result.shape[1:], jnp.bfloat16).at[home_slot].set(result)
    )
    returned = lax.all_to_all(going_back, "req", split_axis=0, concat_axis=0, tiled=True)
    result = jnp.take(returned, arrival_slot, axis=0)
    live_mask = (
        jnp.arange(embedding_per_slot.shape[1], dtype=jnp.int32)[None, :] < tally_per_slot[:, None]
    )
    return jnp.where(live_mask[:, :, None], result, jnp.zeros_like(result))[None]


def solution(mesh):
    return jax.shard_map(
        body,
        mesh=mesh,
        in_specs=(
            P("req", None, "head"),
            P("req"),
            P(),
            P("section", "req", "head", None, None),
            P("section", "req", "head"),
            P("section", None, None),
            P("section", None, "head"),
            P("section", None, "head"),
            P("section", None, "head"),
            P("section", "head", None),
            P("section", "head", None),
            P("section", None, "head"),
            P("section", "head", None),
            P("section", None, "head"),
            P("section", "head"),
            P("section", "head"),
            P("section", "head"),
            P("section", "head"),
            P("section", "head"),
            P("section", "head"),
            P("section", "head"),
        ),
        out_specs=P("section", "req", None, "head"),
        check_vma=False,
    )
```

```python
import jax
import jax.numpy as jnp
from jax import lax
from jax.experimental import pallas as pl
from jax.experimental.pallas import tpu as pltpu
from jax.sharding import PartitionSpec as P

highest = lax.Precision.HIGHEST


def recurrence_kernel(memory_ref, vector_ref, content_ref, read_ref):
    states = memory_ref[...]
    for position in range(vector_ref.shape[0]):
        decay = vector_ref[position, 0]
        normed = vector_ref[position, 1]
        normed_learn = vector_ref[position, 2]
        erasing = vector_ref[position, 3]
        acceptor = vector_ref[position, 4]
        content = content_ref[position]
        pulled = jnp.einsum(
            "bij,bqj->biq", states, normed, precision=lax.Precision.HIGH, preferred_element_type=jnp.float32
        )
        added = jnp.einsum(
            "bqi,bqj->bij", content, erasing, precision=lax.Precision.HIGH, preferred_element_type=jnp.float32
        )
        states = states * decay - pulled * normed_learn + added
        read_ref[position] = jnp.einsum(
            "bqj,bij->bqi", acceptor, states, precision=lax.Precision.HIGH, preferred_element_type=jnp.float32
        )


def run_recurrence(starting_memory, vectors, content):
    steps = vectors.shape[0]
    blocks, span, _ = starting_memory.shape
    return pl.pallas_call(
        recurrence_kernel,
        out_shape=jax.ShapeDtypeStruct((steps, blocks, 1, span), jnp.float32),
        in_specs=[pl.BlockSpec(memory_space=pltpu.VMEM)] * 3,
        out_specs=pl.BlockSpec(memory_space=pltpu.VMEM),
    )(starting_memory, vectors, content)


def sequence_recurrence(
    acceptor_entries,
    address_entries,
    content_entries,
    latent_response,
    adapt_latent,
    starting_memory,
    fading_second_lowrank,
    adapt_second_lowrank,
    fading_baseline,
    adapt_baseline,
    erasing_address_gains,
    address_rate_coupling,
    present_extra_gain,
    section_standard_gains,
    section_standard_shift_terms,
):
    batch_rows = starting_memory.shape[0]
    stored_memory_parts = starting_memory.shape[1]
    subspace_span = starting_memory.shape[2]

    def to_heads(array_in):
        return array_in.reshape(batch_rows, -1, stored_memory_parts, subspace_span)

    log_rate = (
        -jax.nn.softplus(
            -(
                fading_baseline
                + jnp.dot(
                    latent_response, fading_second_lowrank, preferred_element_type=jnp.float32
                )
            )
        )
        - 0.5
    )
    decays = to_heads(jnp.exp(-jnp.exp(log_rate)))
    learning = jax.nn.sigmoid(
        adapt_baseline
        + jnp.dot(adapt_latent, adapt_second_lowrank, preferred_element_type=jnp.float32)
    )
    learn_heads = to_heads(learning)
    scaled = to_heads(address_entries * erasing_address_gains)
    normed = scaled / jnp.sqrt(jnp.sum(scaled * scaled, axis=-1, keepdims=True) + 1e-06)
    erasing_flat = address_entries * (1.0 + (learning - 1.0) * address_rate_coupling)
    erasing_address = to_heads(erasing_flat)
    acceptor_parts = to_heads(acceptor_entries)
    content_part_lines = to_heads(content_entries)
    steps_count = acceptor_parts.shape[1]

    def by_step(array_in):
        return jnp.transpose(array_in, (1, 0, 2, 3)).reshape(
            steps_count, batch_rows * stored_memory_parts, 1, subspace_span
        )

    vectors = jnp.stack(
        [
            by_step(decays),
            by_step(normed),
            by_step(normed * learn_heads),
            by_step(erasing_address),
            by_step(acceptor_parts),
        ],
        axis=1,
    )
    content = by_step(content_part_lines)
    read = run_recurrence(
        starting_memory.reshape(batch_rows * stored_memory_parts, subspace_span, subspace_span),
        vectors,
        content,
    )
    read_all = jnp.transpose(
        read.reshape(steps_count, batch_rows, stored_memory_parts, subspace_span), (1, 0, 2, 3)
    )
    center = read_all - jnp.mean(read_all, axis=-1, keepdims=True)
    variance = jnp.mean(center * center, axis=-1, keepdims=True)
    flat_shape = (batch_rows * acceptor_parts.shape[1], stored_memory_parts * subspace_span)
    standardized_parts = (center / jnp.sqrt(variance + 0.00064)).reshape(
        flat_shape
    ) * section_standard_gains + section_standard_shift_terms
    present_extra_term = (
        jnp.sum(
            to_heads(acceptor_entries * erasing_flat * present_extra_gain),
            axis=-1,
            keepdims=True,
        )
        * content_part_lines
    ).reshape(flat_shape)
    return (standardized_parts + present_extra_term).astype(jnp.bfloat16)


def in_device_order(pieces):
    n = len(pieces)
    me = lax.axis_index("head")
    ordered = []
    for d in range(n):
        chosen = pieces[0]
        for k in range(1, n):
            chosen = jnp.where((me - k) % n == d, pieces[k], chosen)
        ordered.append(chosen)
    return ordered


def gather_heads(block):
    n = lax.axis_size("head")
    pieces = [block]
    for k in range(1, n):
        pieces.append(lax.ppermute(block, "head", [(i, (i + k) % n) for i in range(n)]))
    return in_device_order(pieces)


def scatter_heads(partial):
    n = lax.axis_size("head")
    me = lax.axis_index("head")
    width = partial.shape[1] // n
    total = lax.dynamic_slice_in_dim(partial, me * width, width, 1)
    for k in range(1, n):
        chunk = lax.dynamic_slice_in_dim(partial, ((me + k) % n) * width, width, 1)
        total = total + lax.ppermute(chunk, "head", [(i, (i + k) % n) for i in range(n)])
    return total


def hand_over(partial):
    n = lax.axis_size("head")
    total = None
    for k in range(n):
        piece = lax.ppermute(partial, ("section", "head"), [(i, n + (i + k) % n) for i in range(n)])
        total = piece if total is None else total + piece
    return total


def hand_back(block):
    n = lax.axis_size("head")
    return lax.ppermute(block, ("section", "head"), [(n + i, i) for i in range(n)])


def run_layer(full_now, full_prev_row, params):
    (
        lag_interpolants,
        acceptor_projection,
        address_projection,
        content_projection,
        readout_projection,
        fading_first_full,
        fading_second_lowrank,
        adapt_first_full,
        adapt_second_lowrank,
        fading_baseline,
        adapt_baseline,
        erasing_address_gains,
        address_rate_coupling,
        present_extra_gain,
        section_standard_gains,
        section_standard_shift_terms,
    ) = params
    batch_rows, steps_count, span_width = full_now.shape
    previous = jnp.concatenate([full_prev_row[:, None, :], full_now[:, :-1, :]], axis=1)
    coef_rows = lag_interpolants.astype(jnp.float32)
    current_piece = full_now.astype(jnp.float32)
    spread_piece = previous.astype(jnp.float32) - current_piece
    blends = [
        (current_piece + spread_piece * coef_rows[which_mix])
        .astype(jnp.bfloat16)
        .reshape(-1, span_width)
        for which_mix in range(5)
    ]
    def project(blend, weight):
        return lax.dot_general(
            weight, blend, (((0,), (1,)), ((), ())), preferred_element_type=jnp.float32
        ).T

    acceptor_entries = project(blends[0], acceptor_projection)
    address_entries = project(blends[2], address_projection)
    content_entries = project(blends[3], content_projection)
    latent_response = jnp.tanh(
        jnp.dot(blends[1], fading_first_full, preferred_element_type=jnp.float32)
    ).astype(jnp.bfloat16)
    adapt_latent = jnp.dot(blends[4], adapt_first_full, preferred_element_type=jnp.float32).astype(
        jnp.bfloat16
    )
    return acceptor_entries, address_entries, content_entries, latent_response, adapt_latent


def layer_partial(full_now, full_prev_row, starting_memory, params):
    entries = run_layer(full_now, full_prev_row, params)
    lagged_features = sequence_recurrence(
        *entries,
        starting_memory,
        params[6],
        params[8],
        *params[9:],
    )
    return jnp.dot(lagged_features, params[4], preferred_element_type=jnp.float32)


def run_sections(inputs, states_use, last_use, params):
    section_num = lax.axis_index("section")
    n = lax.axis_size("head")
    batch_rows, steps_count, shard_width = inputs.shape
    fading_first, adapt_first = params[5], params[7]
    sizes = [inputs.size, last_use.size, fading_first.size, adapt_first.size]
    packed = jnp.concatenate(
        [inputs.reshape(-1), last_use.reshape(-1), fading_first.reshape(-1), adapt_first.reshape(-1)]
    )
    ordered = gather_heads(packed)
    cuts = [0]
    for size in sizes:
        cuts.append(cuts[-1] + size)

    def joined(index, shape, axis):
        parts = [piece[cuts[index] : cuts[index + 1]].reshape(shape) for piece in ordered]
        return jnp.concatenate(parts, axis=axis)

    full_first = joined(0, inputs.shape, 2)
    full_prev = joined(1, last_use.shape, 1)
    fading_full = joined(2, fading_first.shape, 0)
    adapt_full = joined(3, adapt_first.shape, 0)
    params = params[:5] + (fading_full, params[6], adapt_full) + params[8:]
    partial_first = layer_partial(full_first, full_prev, states_use, params)
    total_first = hand_over(partial_first)
    full_second = (
        full_first.astype(jnp.float32) + total_first.reshape(full_first.shape)
    ).astype(jnp.bfloat16)
    me = lax.axis_index("head")
    second_in = lax.dynamic_slice_in_dim(full_second, me * shard_width, shard_width, 2)
    first_out = hand_back(second_in)
    partial_second = layer_partial(full_second, full_prev, states_use, params)
    own_second = scatter_heads(partial_second).reshape(batch_rows, steps_count, shard_width)
    second_out = (second_in.astype(jnp.float32) + own_second).astype(jnp.bfloat16)
    return jnp.where(section_num == 0, first_out, second_out)


def body(
    embedding_per_slot,
    tally_per_slot,
    slot_requests,
    memory_per_request,
    previous_step_feature,
    lag_interpolants,
    acceptor_projection,
    address_projection,
    content_projection,
    readout_projection,
    fading_first_lowrank,
    fading_second_lowrank,
    adapt_first_lowrank,
    adapt_second_lowrank,
    fading_baseline,
    adapt_baseline,
    erasing_address_gains,
    address_rate_coupling,
    present_extra_gain,
    section_standard_gains,
    section_standard_shift_terms,
):
    local_rows = embedding_per_slot.shape[0]
    groups = lax.axis_size("req")
    capacity = (local_rows + groups - 1) // groups
    my_group = lax.axis_index("req")
    slot_ids = jnp.arange(local_rows, dtype=jnp.int32)
    table = slot_requests.reshape(groups, local_rows)
    my_arrivals = lax.dynamic_index_in_dim(table, my_group, 0, keepdims=False)
    home_group = my_arrivals // local_rows
    earlier = slot_ids[None, :] < slot_ids[:, None]
    arrival_rank = jnp.sum(
        ((home_group[:, None] == home_group[None, :]) & earlier).astype(jnp.int32), axis=1
    )
    arrival_slot = home_group * capacity + arrival_rank
    requests = my_group * local_rows + slot_ids
    total_rows = slot_requests.shape[0]
    found = slot_requests[None, :] == requests[:, None]
    positions = jnp.sum(
        jnp.where(found, jnp.arange(total_rows, dtype=jnp.int32)[None, :], 0), axis=1
    )
    source = positions // local_rows
    within = positions % local_rows
    source_homes = jnp.take(table, source, axis=0) // local_rows
    home_rank = jnp.sum(
        ((source_homes == my_group) & (slot_ids[None, :] < within[:, None])).astype(jnp.int32),
        axis=1,
    )
    home_slot = source * capacity + home_rank
    buffer_rows = groups * capacity
    params = (
        lag_interpolants.reshape(lag_interpolants.shape[1:]),
        acceptor_projection.reshape(acceptor_projection.shape[1:]),
        address_projection.reshape(address_projection.shape[1:]),
        content_projection.reshape(content_projection.shape[1:]),
        readout_projection.reshape(readout_projection.shape[1:]),
        fading_first_lowrank.reshape(fading_first_lowrank.shape[1:]),
        fading_second_lowrank.reshape(fading_second_lowrank.shape[1:]),
        adapt_first_lowrank.reshape(adapt_first_lowrank.shape[1:]),
        adapt_second_lowrank.reshape(adapt_second_lowrank.shape[1:]),
        fading_baseline,
        adapt_baseline,
        erasing_address_gains,
        address_rate_coupling,
        present_extra_gain,
        section_standard_gains,
        section_standard_shift_terms,
    )
    states_local = memory_per_request.reshape(memory_per_request.shape[1:])
    last_local = previous_step_feature.reshape(previous_step_feature.shape[1:])
    outgoing = (
        jnp.zeros((buffer_rows,) + embedding_per_slot.shape[1:], jnp.bfloat16)
        .at[arrival_slot]
        .set(embedding_per_slot)
    )
    arrived = lax.all_to_all(outgoing, "req", split_axis=0, concat_axis=0, tiled=True)
    inputs = jnp.take(arrived, home_slot, axis=0)
    result = run_sections(inputs, states_local, last_local, params)
    going_back = (
        jnp.zeros((buffer_rows,) + result.shape[1:], jnp.bfloat16).at[home_slot].set(result)
    )
    returned = lax.all_to_all(going_back, "req", split_axis=0, concat_axis=0, tiled=True)
    result = jnp.take(returned, arrival_slot, axis=0)
    live_mask = (
        jnp.arange(embedding_per_slot.shape[1], dtype=jnp.int32)[None, :] < tally_per_slot[:, None]
    )
    return jnp.where(live_mask[:, :, None], result, jnp.zeros_like(result))[None]


def solution(mesh):
    return jax.shard_map(
        body,
        mesh=mesh,
        in_specs=(
            P("req", None, "head"),
            P("req"),
            P(),
            P("section", "req", "head", None, None),
            P("section", "req", "head"),
            P("section", None, None),
            P("section", None, "head"),
            P("section", None, "head"),
            P("section", None, "head"),
            P("section", "head", None),
            P("section", "head", None),
            P("section", None, "head"),
            P("section", "head", None),
            P("section", None, "head"),
            P("section", "head"),
            P("section", "head"),
            P("section", "head"),
            P("section", "head"),
            P("section", "head"),
            P("section", "head"),
            P("section", "head"),
        ),
        out_specs=P("section", "req", None, "head"),
        check_vma=False,
    )
```

```python
import jax
import jax.numpy as jnp
from jax import lax
from jax.experimental import pallas as pl
from jax.experimental.pallas import tpu as pltpu
from jax.sharding import PartitionSpec as P

highest = lax.Precision.HIGHEST


def recurrence_kernel(memory_ref, vector_ref, content_ref, read_ref):
    states = memory_ref[...]
    for position in range(vector_ref.shape[0]):
        decay = vector_ref[position, 0]
        normed = vector_ref[position, 1]
        normed_learn = vector_ref[position, 2]
        erasing = vector_ref[position, 3]
        acceptor = vector_ref[position, 4]
        content = content_ref[position]
        pulled = jnp.sum(states * normed, axis=-1, keepdims=True)
        added = jnp.einsum(
            "bqi,bqj->bij", content, erasing, precision=lax.Precision.HIGH, preferred_element_type=jnp.float32
        )
        states = states * decay - pulled * normed_learn + added
        read_ref[position] = jnp.einsum(
            "bqj,bij->bqi", acceptor, states, precision=lax.Precision.HIGH, preferred_element_type=jnp.float32
        )


def run_recurrence(starting_memory, vectors, content):
    steps = vectors.shape[0]
    blocks, span, _ = starting_memory.shape
    return pl.pallas_call(
        recurrence_kernel,
        out_shape=jax.ShapeDtypeStruct((steps, blocks, 1, span), jnp.float32),
        in_specs=[pl.BlockSpec(memory_space=pltpu.VMEM)] * 3,
        out_specs=pl.BlockSpec(memory_space=pltpu.VMEM),
    )(starting_memory, vectors, content)


def sequence_recurrence(
    acceptor_entries,
    address_entries,
    content_entries,
    latent_response,
    adapt_latent,
    starting_memory,
    fading_second_lowrank,
    adapt_second_lowrank,
    fading_baseline,
    adapt_baseline,
    erasing_address_gains,
    address_rate_coupling,
    present_extra_gain,
    section_standard_gains,
    section_standard_shift_terms,
):
    batch_rows = starting_memory.shape[0]
    stored_memory_parts = starting_memory.shape[1]
    subspace_span = starting_memory.shape[2]

    def to_heads(array_in):
        return array_in.reshape(batch_rows, -1, stored_memory_parts, subspace_span)

    log_rate = (
        -jax.nn.softplus(
            -(
                fading_baseline
                + jnp.dot(
                    latent_response, fading_second_lowrank, preferred_element_type=jnp.float32
                )
            )
        )
        - 0.5
    )
    decays = to_heads(jnp.exp(-jnp.exp(log_rate)))
    learning = jax.nn.sigmoid(
        adapt_baseline
        + jnp.dot(adapt_latent, adapt_second_lowrank, preferred_element_type=jnp.float32)
    )
    learn_heads = to_heads(learning)
    scaled = to_heads(address_entries * erasing_address_gains)
    normed = scaled / jnp.sqrt(jnp.sum(scaled * scaled, axis=-1, keepdims=True) + 1e-06)
    erasing_flat = address_entries * (1.0 + (learning - 1.0) * address_rate_coupling)
    erasing_address = to_heads(erasing_flat)
    acceptor_parts = to_heads(acceptor_entries)
    content_part_lines = to_heads(content_entries)
    steps_count = acceptor_parts.shape[1]

    def by_step(array_in):
        return jnp.transpose(array_in, (1, 0, 2, 3)).reshape(
            steps_count, batch_rows * stored_memory_parts, 1, subspace_span
        )

    vectors = jnp.stack(
        [
            by_step(decays),
            by_step(normed),
            by_step(normed * learn_heads),
            by_step(erasing_address),
            by_step(acceptor_parts),
        ],
        axis=1,
    )
    content = by_step(content_part_lines)
    read = run_recurrence(
        starting_memory.reshape(batch_rows * stored_memory_parts, subspace_span, subspace_span),
        vectors,
        content,
    )
    read_all = jnp.transpose(
        read.reshape(steps_count, batch_rows, stored_memory_parts, subspace_span), (1, 0, 2, 3)
    )
    center = read_all - jnp.mean(read_all, axis=-1, keepdims=True)
    variance = jnp.mean(center * center, axis=-1, keepdims=True)
    flat_shape = (batch_rows * acceptor_parts.shape[1], stored_memory_parts * subspace_span)
    standardized_parts = (center / jnp.sqrt(variance + 0.00064)).reshape(
        flat_shape
    ) * section_standard_gains + section_standard_shift_terms
    present_extra_term = (
        jnp.sum(
            to_heads(acceptor_entries * erasing_flat * present_extra_gain),
            axis=-1,
            keepdims=True,
        )
        * content_part_lines
    ).reshape(flat_shape)
    return (standardized_parts + present_extra_term).astype(jnp.bfloat16)


def in_device_order(pieces):
    n = len(pieces)
    me = lax.axis_index("head")
    ordered = []
    for d in range(n):
        chosen = pieces[0]
        for k in range(1, n):
            chosen = jnp.where((me - k) % n == d, pieces[k], chosen)
        ordered.append(chosen)
    return ordered


def gather_heads(block):
    n = lax.axis_size("head")
    pieces = [block]
    for k in range(1, n):
        pieces.append(lax.ppermute(block, "head", [(i, (i + k) % n) for i in range(n)]))
    return in_device_order(pieces)


def scatter_heads(partial):
    n = lax.axis_size("head")
    me = lax.axis_index("head")
    width = partial.shape[1] // n
    total = lax.dynamic_slice_in_dim(partial, me * width, width, 1)
    for k in range(1, n):
        chunk = lax.dynamic_slice_in_dim(partial, ((me + k) % n) * width, width, 1)
        total = total + lax.ppermute(chunk, "head", [(i, (i + k) % n) for i in range(n)])
    return total


def hand_over(partial):
    n = lax.axis_size("head")
    total = None
    for k in range(n):
        piece = lax.ppermute(partial, ("section", "head"), [(i, n + (i + k) % n) for i in range(n)])
        total = piece if total is None else total + piece
    return total


def hand_back(block):
    n = lax.axis_size("head")
    return lax.ppermute(block, ("section", "head"), [(n + i, i) for i in range(n)])


def run_layer(full_now, full_prev_row, params):
    (
        lag_interpolants,
        acceptor_projection,
        address_projection,
        content_projection,
        readout_projection,
        fading_first_full,
        fading_second_lowrank,
        adapt_first_full,
        adapt_second_lowrank,
        fading_baseline,
        adapt_baseline,
        erasing_address_gains,
        address_rate_coupling,
        present_extra_gain,
        section_standard_gains,
        section_standard_shift_terms,
    ) = params
    batch_rows, steps_count, span_width = full_now.shape
    previous = jnp.concatenate([full_prev_row[:, None, :], full_now[:, :-1, :]], axis=1)
    coef_rows = lag_interpolants.astype(jnp.float32)
    current_piece = full_now.astype(jnp.float32)
    spread_piece = previous.astype(jnp.float32) - current_piece
    blends = [
        (current_piece + spread_piece * coef_rows[which_mix])
        .astype(jnp.bfloat16)
        .reshape(-1, span_width)
        for which_mix in range(5)
    ]
    def project(blend, weight):
        return lax.dot_general(
            weight, blend, (((0,), (1,)), ((), ())), preferred_element_type=jnp.float32
        ).T

    acceptor_entries = project(blends[0], acceptor_projection)
    address_entries = project(blends[2], address_projection)
    content_entries = project(blends[3], content_projection)
    latent_response = jnp.tanh(
        jnp.dot(blends[1], fading_first_full, preferred_element_type=jnp.float32)
    ).astype(jnp.bfloat16)
    adapt_latent = jnp.dot(blends[4], adapt_first_full, preferred_element_type=jnp.float32).astype(
        jnp.bfloat16
    )
    return acceptor_entries, address_entries, content_entries, latent_response, adapt_latent


def layer_partial(full_now, full_prev_row, starting_memory, params):
    entries = run_layer(full_now, full_prev_row, params)
    lagged_features = sequence_recurrence(
        *entries,
        starting_memory,
        params[6],
        params[8],
        *params[9:],
    )
    return jnp.dot(lagged_features, params[4], preferred_element_type=jnp.float32)


def run_sections(inputs, states_use, last_use, params):
    section_num = lax.axis_index("section")
    n = lax.axis_size("head")
    batch_rows, steps_count, shard_width = inputs.shape
    fading_first, adapt_first = params[5], params[7]
    sizes = [inputs.size, last_use.size, fading_first.size, adapt_first.size]
    packed = jnp.concatenate(
        [inputs.reshape(-1), last_use.reshape(-1), fading_first.reshape(-1), adapt_first.reshape(-1)]
    )
    ordered = gather_heads(packed)
    cuts = [0]
    for size in sizes:
        cuts.append(cuts[-1] + size)

    def joined(index, shape, axis):
        parts = [piece[cuts[index] : cuts[index + 1]].reshape(shape) for piece in ordered]
        return jnp.concatenate(parts, axis=axis)

    full_first = joined(0, inputs.shape, 2)
    full_prev = joined(1, last_use.shape, 1)
    fading_full = joined(2, fading_first.shape, 0)
    adapt_full = joined(3, adapt_first.shape, 0)
    params = params[:5] + (fading_full, params[6], adapt_full) + params[8:]
    partial_first = layer_partial(full_first, full_prev, states_use, params)
    total_first = hand_over(partial_first)
    full_second = (
        full_first.astype(jnp.float32) + total_first.reshape(full_first.shape)
    ).astype(jnp.bfloat16)
    me = lax.axis_index("head")
    second_in = lax.dynamic_slice_in_dim(full_second, me * shard_width, shard_width, 2)
    first_out = hand_back(second_in)
    partial_second = layer_partial(full_second, full_prev, states_use, params)
    own_second = scatter_heads(partial_second).reshape(batch_rows, steps_count, shard_width)
    second_out = (second_in.astype(jnp.float32) + own_second).astype(jnp.bfloat16)
    return jnp.where(section_num == 0, first_out, second_out)


def place_rows(rows, index, count):
    found = index[None, :] == jnp.arange(count, dtype=jnp.int32)[:, None]
    source = jnp.sum(
        jnp.where(found, jnp.arange(index.shape[0], dtype=jnp.int32)[None, :], 0), axis=1
    )
    present = jnp.any(found, axis=1)
    picked = jnp.take(rows, source, axis=0)
    return jnp.where(present.reshape((count,) + (1,) * (rows.ndim - 1)), picked, jnp.zeros_like(picked))


def body(
    embedding_per_slot,
    tally_per_slot,
    slot_requests,
    memory_per_request,
    previous_step_feature,
    lag_interpolants,
    acceptor_projection,
    address_projection,
    content_projection,
    readout_projection,
    fading_first_lowrank,
    fading_second_lowrank,
    adapt_first_lowrank,
    adapt_second_lowrank,
    fading_baseline,
    adapt_baseline,
    erasing_address_gains,
    address_rate_coupling,
    present_extra_gain,
    section_standard_gains,
    section_standard_shift_terms,
):
    local_rows = embedding_per_slot.shape[0]
    groups = lax.axis_size("req")
    capacity = (local_rows + groups - 1) // groups
    my_group = lax.axis_index("req")
    slot_ids = jnp.arange(local_rows, dtype=jnp.int32)
    table = slot_requests.reshape(groups, local_rows)
    my_arrivals = lax.dynamic_index_in_dim(table, my_group, 0, keepdims=False)
    home_group = my_arrivals // local_rows
    earlier = slot_ids[None, :] < slot_ids[:, None]
    arrival_rank = jnp.sum(
        ((home_group[:, None] == home_group[None, :]) & earlier).astype(jnp.int32), axis=1
    )
    arrival_slot = home_group * capacity + arrival_rank
    requests = my_group * local_rows + slot_ids
    total_rows = slot_requests.shape[0]
    found = slot_requests[None, :] == requests[:, None]
    positions = jnp.sum(
        jnp.where(found, jnp.arange(total_rows, dtype=jnp.int32)[None, :], 0), axis=1
    )
    source = positions // local_rows
    within = positions % local_rows
    source_homes = jnp.take(table, source, axis=0) // local_rows
    home_rank = jnp.sum(
        ((source_homes == my_group) & (slot_ids[None, :] < within[:, None])).astype(jnp.int32),
        axis=1,
    )
    home_slot = source * capacity + home_rank
    buffer_rows = groups * capacity
    params = (
        lag_interpolants.reshape(lag_interpolants.shape[1:]),
        acceptor_projection.reshape(acceptor_projection.shape[1:]),
        address_projection.reshape(address_projection.shape[1:]),
        content_projection.reshape(content_projection.shape[1:]),
        readout_projection.reshape(readout_projection.shape[1:]),
        fading_first_lowrank.reshape(fading_first_lowrank.shape[1:]),
        fading_second_lowrank.reshape(fading_second_lowrank.shape[1:]),
        adapt_first_lowrank.reshape(adapt_first_lowrank.shape[1:]),
        adapt_second_lowrank.reshape(adapt_second_lowrank.shape[1:]),
        fading_baseline,
        adapt_baseline,
        erasing_address_gains,
        address_rate_coupling,
        present_extra_gain,
        section_standard_gains,
        section_standard_shift_terms,
    )
    states_local = memory_per_request.reshape(memory_per_request.shape[1:])
    last_local = previous_step_feature.reshape(previous_step_feature.shape[1:])
    outgoing = place_rows(embedding_per_slot, arrival_slot, buffer_rows)
    arrived = lax.all_to_all(outgoing, "req", split_axis=0, concat_axis=0, tiled=True)
    inputs = jnp.take(arrived, home_slot, axis=0)
    result = run_sections(inputs, states_local, last_local, params)
    going_back = place_rows(result, home_slot, buffer_rows)
    returned = lax.all_to_all(going_back, "req", split_axis=0, concat_axis=0, tiled=True)
    result = jnp.take(returned, arrival_slot, axis=0)
    live_mask = (
        jnp.arange(embedding_per_slot.shape[1], dtype=jnp.int32)[None, :] < tally_per_slot[:, None]
    )
    return jnp.where(live_mask[:, :, None], result, jnp.zeros_like(result))[None]


def solution(mesh):
    return jax.shard_map(
        body,
        mesh=mesh,
        in_specs=(
            P("req", None, "head"),
            P("req"),
            P(),
            P("section", "req", "head", None, None),
            P("section", "req", "head"),
            P("section", None, None),
            P("section", None, "head"),
            P("section", None, "head"),
            P("section", None, "head"),
            P("section", "head", None),
            P("section", "head", None),
            P("section", None, "head"),
            P("section", "head", None),
            P("section", None, "head"),
            P("section", "head"),
            P("section", "head"),
            P("section", "head"),
            P("section", "head"),
            P("section", "head"),
            P("section", "head"),
            P("section", "head"),
        ),
        out_specs=P("section", "req", None, "head"),
        check_vma=False,
    )
```

```python
import jax
import jax.numpy as jnp
from jax import lax
from jax.experimental import pallas as pl
from jax.experimental.pallas import tpu as pltpu
from jax.sharding import PartitionSpec as P

highest = lax.Precision.HIGHEST


def recurrence_kernel(memory_ref, vector_ref, content_ref, read_ref):
    states = memory_ref[...]
    for position in range(vector_ref.shape[0]):
        decay = vector_ref[position, 0]
        normed = vector_ref[position, 1]
        normed_learn = vector_ref[position, 2]
        erasing = vector_ref[position, 3]
        acceptor = vector_ref[position, 4]
        content = content_ref[position]
        pulled = jnp.sum(states * normed, axis=-1, keepdims=True)
        added = jnp.einsum(
            "bqi,bqj->bij", content, erasing, precision=lax.Precision.HIGH, preferred_element_type=jnp.float32
        )
        states = states * decay - pulled * normed_learn + added
        read_ref[position] = jnp.einsum(
            "bqj,bij->bqi", acceptor, states, precision=lax.Precision.HIGH, preferred_element_type=jnp.float32
        )


def run_recurrence(starting_memory, vectors, content):
    steps = vectors.shape[0]
    blocks, span, _ = starting_memory.shape
    return pl.pallas_call(
        recurrence_kernel,
        out_shape=jax.ShapeDtypeStruct((steps, blocks, 1, span), jnp.float32),
        in_specs=[pl.BlockSpec(memory_space=pltpu.VMEM)] * 3,
        out_specs=pl.BlockSpec(memory_space=pltpu.VMEM),
    )(starting_memory, vectors, content)


def sequence_recurrence(
    acceptor_entries,
    address_entries,
    content_entries,
    latent_response,
    adapt_latent,
    starting_memory,
    fading_second_lowrank,
    adapt_second_lowrank,
    fading_baseline,
    adapt_baseline,
    erasing_address_gains,
    address_rate_coupling,
    present_extra_gain,
    section_standard_gains,
    section_standard_shift_terms,
):
    batch_rows = starting_memory.shape[0]
    stored_memory_parts = starting_memory.shape[1]
    subspace_span = starting_memory.shape[2]

    def to_heads(array_in):
        return array_in.reshape(batch_rows, -1, stored_memory_parts, subspace_span)

    log_rate = (
        -jax.nn.softplus(
            -(
                fading_baseline
                + jnp.dot(
                    latent_response, fading_second_lowrank, preferred_element_type=jnp.float32
                )
            )
        )
        - 0.5
    )
    decays = to_heads(jnp.exp(-jnp.exp(log_rate)))
    learning = jax.nn.sigmoid(
        adapt_baseline
        + jnp.dot(adapt_latent, adapt_second_lowrank, preferred_element_type=jnp.float32)
    )
    learn_heads = to_heads(learning)
    scaled = to_heads(address_entries * erasing_address_gains)
    normed = scaled / jnp.sqrt(jnp.sum(scaled * scaled, axis=-1, keepdims=True) + 1e-06)
    erasing_flat = address_entries * (1.0 + (learning - 1.0) * address_rate_coupling)
    erasing_address = to_heads(erasing_flat)
    acceptor_parts = to_heads(acceptor_entries)
    content_part_lines = to_heads(content_entries)
    steps_count = acceptor_parts.shape[1]

    def by_step(array_in):
        return jnp.transpose(array_in, (1, 0, 2, 3)).reshape(
            steps_count, batch_rows * stored_memory_parts, 1, subspace_span
        )

    vectors = jnp.stack(
        [
            by_step(decays),
            by_step(normed),
            by_step(normed * learn_heads),
            by_step(erasing_address),
            by_step(acceptor_parts),
        ],
        axis=1,
    )
    content = by_step(content_part_lines)
    read = run_recurrence(
        starting_memory.reshape(batch_rows * stored_memory_parts, subspace_span, subspace_span),
        vectors,
        content,
    )
    read_all = jnp.transpose(
        read.reshape(steps_count, batch_rows, stored_memory_parts, subspace_span), (1, 0, 2, 3)
    )
    center = read_all - jnp.mean(read_all, axis=-1, keepdims=True)
    variance = jnp.mean(center * center, axis=-1, keepdims=True)
    flat_shape = (batch_rows * acceptor_parts.shape[1], stored_memory_parts * subspace_span)
    standardized_parts = (center / jnp.sqrt(variance + 0.00064)).reshape(
        flat_shape
    ) * section_standard_gains + section_standard_shift_terms
    present_extra_term = (
        jnp.sum(
            to_heads(acceptor_entries * erasing_flat * present_extra_gain),
            axis=-1,
            keepdims=True,
        )
        * content_part_lines
    ).reshape(flat_shape)
    return (standardized_parts + present_extra_term).astype(jnp.bfloat16)


def in_device_order(pieces):
    n = len(pieces)
    me = lax.axis_index("head")
    ordered = []
    for d in range(n):
        chosen = pieces[0]
        for k in range(1, n):
            chosen = jnp.where((me - k) % n == d, pieces[k], chosen)
        ordered.append(chosen)
    return ordered


def gather_heads(block):
    n = lax.axis_size("head")
    pieces = [block]
    for k in range(1, n):
        pieces.append(lax.ppermute(block, "head", [(i, (i + k) % n) for i in range(n)]))
    return in_device_order(pieces)


def scatter_heads(partial):
    n = lax.axis_size("head")
    me = lax.axis_index("head")
    width = partial.shape[1] // n
    total = lax.dynamic_slice_in_dim(partial, me * width, width, 1)
    for k in range(1, n):
        chunk = lax.dynamic_slice_in_dim(partial, ((me + k) % n) * width, width, 1)
        total = total + lax.ppermute(chunk, "head", [(i, (i + k) % n) for i in range(n)])
    return total


def hand_over(partial):
    n = lax.axis_size("head")
    total = None
    for k in range(n):
        piece = lax.ppermute(partial, ("section", "head"), [(i, n + (i + k) % n) for i in range(n)])
        total = piece if total is None else total + piece
    return total


def hand_back(block):
    n = lax.axis_size("head")
    return lax.ppermute(block, ("section", "head"), [(n + i, i) for i in range(n)])


def run_layer(full_now, full_prev_row, params):
    (
        lag_interpolants,
        acceptor_projection,
        address_projection,
        content_projection,
        readout_projection,
        fading_first_full,
        fading_second_lowrank,
        adapt_first_full,
        adapt_second_lowrank,
        fading_baseline,
        adapt_baseline,
        erasing_address_gains,
        address_rate_coupling,
        present_extra_gain,
        section_standard_gains,
        section_standard_shift_terms,
    ) = params
    batch_rows, steps_count, span_width = full_now.shape
    previous = jnp.concatenate([full_prev_row[:, None, :], full_now[:, :-1, :]], axis=1)
    coef_rows = lag_interpolants.astype(jnp.float32)
    current_piece = full_now.astype(jnp.float32)
    spread_piece = previous.astype(jnp.float32) - current_piece
    blends = [
        (current_piece + spread_piece * coef_rows[which_mix])
        .astype(jnp.bfloat16)
        .reshape(-1, span_width)
        for which_mix in range(5)
    ]
    def project(blend, weight):
        return lax.dot_general(
            weight, blend, (((0,), (1,)), ((), ())), preferred_element_type=jnp.float32
        ).T

    acceptor_entries = project(blends[0], acceptor_projection)
    address_entries = project(blends[2], address_projection)
    content_entries = project(blends[3], content_projection)
    latent_response = jnp.tanh(
        jnp.dot(blends[1], fading_first_full, preferred_element_type=jnp.float32)
    ).astype(jnp.bfloat16)
    adapt_latent = jnp.dot(blends[4], adapt_first_full, preferred_element_type=jnp.float32).astype(
        jnp.bfloat16
    )
    return acceptor_entries, address_entries, content_entries, latent_response, adapt_latent


def layer_partial(full_now, full_prev_row, starting_memory, params):
    entries = run_layer(full_now, full_prev_row, params)
    lagged_features = sequence_recurrence(
        *entries,
        starting_memory,
        params[6],
        params[8],
        *params[9:],
    )
    return jnp.dot(lagged_features, params[4], preferred_element_type=jnp.float32)


def run_sections(inputs, states_use, last_use, params):
    section_num = lax.axis_index("section")
    n = lax.axis_size("head")
    batch_rows, steps_count, shard_width = inputs.shape
    fading_first, adapt_first = params[5], params[7]
    sizes = [inputs.size, last_use.size, fading_first.size, adapt_first.size]
    packed = jnp.concatenate(
        [inputs.reshape(-1), last_use.reshape(-1), fading_first.reshape(-1), adapt_first.reshape(-1)]
    )
    ordered = gather_heads(packed)
    cuts = [0]
    for size in sizes:
        cuts.append(cuts[-1] + size)

    def joined(index, shape, axis):
        parts = [piece[cuts[index] : cuts[index + 1]].reshape(shape) for piece in ordered]
        return jnp.concatenate(parts, axis=axis)

    full_first = joined(0, inputs.shape, 2)
    full_prev = joined(1, last_use.shape, 1)
    fading_full = joined(2, fading_first.shape, 0)
    adapt_full = joined(3, adapt_first.shape, 0)
    params = params[:5] + (fading_full, params[6], adapt_full) + params[8:]
    partial_first = layer_partial(full_first, full_prev, states_use, params)
    total_first = hand_over(partial_first)
    full_second = (
        full_first.astype(jnp.float32) + total_first.reshape(full_first.shape)
    ).astype(jnp.bfloat16)
    me = lax.axis_index("head")
    second_in = lax.dynamic_slice_in_dim(full_second, me * shard_width, shard_width, 2)
    first_out = hand_back(second_in)
    full_second, first_out = lax.optimization_barrier((full_second, first_out))
    partial_second = layer_partial(full_second, full_prev, states_use, params)
    own_second = scatter_heads(partial_second).reshape(batch_rows, steps_count, shard_width)
    second_out = (second_in.astype(jnp.float32) + own_second).astype(jnp.bfloat16)
    return jnp.where(section_num == 0, first_out, second_out)


def body(
    embedding_per_slot,
    tally_per_slot,
    slot_requests,
    memory_per_request,
    previous_step_feature,
    lag_interpolants,
    acceptor_projection,
    address_projection,
    content_projection,
    readout_projection,
    fading_first_lowrank,
    fading_second_lowrank,
    adapt_first_lowrank,
    adapt_second_lowrank,
    fading_baseline,
    adapt_baseline,
    erasing_address_gains,
    address_rate_coupling,
    present_extra_gain,
    section_standard_gains,
    section_standard_shift_terms,
):
    local_rows = embedding_per_slot.shape[0]
    groups = lax.axis_size("req")
    capacity = (local_rows + groups - 1) // groups
    my_group = lax.axis_index("req")
    slot_ids = jnp.arange(local_rows, dtype=jnp.int32)
    table = slot_requests.reshape(groups, local_rows)
    my_arrivals = lax.dynamic_index_in_dim(table, my_group, 0, keepdims=False)
    home_group = my_arrivals // local_rows
    earlier = slot_ids[None, :] < slot_ids[:, None]
    arrival_rank = jnp.sum(
        ((home_group[:, None] == home_group[None, :]) & earlier).astype(jnp.int32), axis=1
    )
    arrival_slot = home_group * capacity + arrival_rank
    requests = my_group * local_rows + slot_ids
    total_rows = slot_requests.shape[0]
    found = slot_requests[None, :] == requests[:, None]
    positions = jnp.sum(
        jnp.where(found, jnp.arange(total_rows, dtype=jnp.int32)[None, :], 0), axis=1
    )
    source = positions // local_rows
    within = positions % local_rows
    source_homes = jnp.take(table, source, axis=0) // local_rows
    home_rank = jnp.sum(
        ((source_homes == my_group) & (slot_ids[None, :] < within[:, None])).astype(jnp.int32),
        axis=1,
    )
    home_slot = source * capacity + home_rank
    buffer_rows = groups * capacity
    params = (
        lag_interpolants.reshape(lag_interpolants.shape[1:]),
        acceptor_projection.reshape(acceptor_projection.shape[1:]),
        address_projection.reshape(address_projection.shape[1:]),
        content_projection.reshape(content_projection.shape[1:]),
        readout_projection.reshape(readout_projection.shape[1:]),
        fading_first_lowrank.reshape(fading_first_lowrank.shape[1:]),
        fading_second_lowrank.reshape(fading_second_lowrank.shape[1:]),
        adapt_first_lowrank.reshape(adapt_first_lowrank.shape[1:]),
        adapt_second_lowrank.reshape(adapt_second_lowrank.shape[1:]),
        fading_baseline,
        adapt_baseline,
        erasing_address_gains,
        address_rate_coupling,
        present_extra_gain,
        section_standard_gains,
        section_standard_shift_terms,
    )
    states_local = memory_per_request.reshape(memory_per_request.shape[1:])
    last_local = previous_step_feature.reshape(previous_step_feature.shape[1:])
    outgoing = (
        jnp.zeros((buffer_rows,) + embedding_per_slot.shape[1:], jnp.bfloat16)
        .at[arrival_slot]
        .set(embedding_per_slot)
    )
    arrived = lax.all_to_all(outgoing, "req", split_axis=0, concat_axis=0, tiled=True)
    inputs = jnp.take(arrived, home_slot, axis=0)
    result = run_sections(inputs, states_local, last_local, params)
    going_back = (
        jnp.zeros((buffer_rows,) + result.shape[1:], jnp.bfloat16).at[home_slot].set(result)
    )
    returned = lax.all_to_all(going_back, "req", split_axis=0, concat_axis=0, tiled=True)
    result = jnp.take(returned, arrival_slot, axis=0)
    live_mask = (
        jnp.arange(embedding_per_slot.shape[1], dtype=jnp.int32)[None, :] < tally_per_slot[:, None]
    )
    return jnp.where(live_mask[:, :, None], result, jnp.zeros_like(result))[None]


def solution(mesh):
    return jax.shard_map(
        body,
        mesh=mesh,
        in_specs=(
            P("req", None, "head"),
            P("req"),
            P(),
            P("section", "req", "head", None, None),
            P("section", "req", "head"),
            P("section", None, None),
            P("section", None, "head"),
            P("section", None, "head"),
            P("section", None, "head"),
            P("section", "head", None),
            P("section", "head", None),
            P("section", None, "head"),
            P("section", "head", None),
            P("section", None, "head"),
            P("section", "head"),
            P("section", "head"),
            P("section", "head"),
            P("section", "head"),
            P("section", "head"),
            P("section", "head"),
            P("section", "head"),
        ),
        out_specs=P("section", "req", None, "head"),
        check_vma=False,
    )
```
